256 devices in a mesh: fsdp: 64 (over x_lo, z, y), dp: 4 (over x_hi, core).
Axes of the slice: x: 4 (x_hi: 2, x_lo: 2; x = x_hi * 2 + x_lo), y: 4, z: 8, core: 2. Of those that a mesh axis runs over, the one named last changes fastest.
Arguments:
- tokens: bfloat16 [4, 8192, 8192], P('dp', 'fsdp'), may hold values from -6 to 6
- queries: bfloat16 [4, 8192, 4096], P('dp', 'fsdp'), may hold values from -40 to 40, as said below
- keys: bfloat16 [4, 8192, 512], P('dp', 'fsdp'), may hold values from -4 to 4
- memory: bfloat16 [4, 8192, 8192], P('dp', 'fsdp'), may hold values from -6 to 6
- mem_keys: bfloat16 [4, 8192, 512], P('dp', 'fsdp'), may hold values from -4 to 4
- cotangent: bfloat16 [4, 8192, 4096], P('dp', 'fsdp'), may hold values from -6 to 6
- value_weight: bfloat16 [8192, 512], P('fsdp'), may hold values from -0.0625 to 0.0625
- dest_group: int32 [4, 128], P('dp', 'fsdp'), may hold values from 0 to 3, as said below
- source_group: int32 [4, 128], P('dp', 'fsdp'), may hold values from 0 to 3, as said below
- lengths: int32 [4, 128], P('dp', 'fsdp'), may hold values from 1 to 64
Outputs:
- grad_queries: bfloat16 [4, 8192, 4096], P('dp', 'fsdp')
- grad_keys: bfloat16 [4, 8192, 512], P('dp', 'fsdp')
- grad_memory: bfloat16 [4, 8192, 8192], P('dp', 'fsdp')
- grad_mem_keys: bfloat16 [4, 8192, 512], P('dp', 'fsdp')
- grad_weight: bfloat16 [8192, 512], P('fsdp')
The draws below stay inside these ranges and needn't reach their ends.
Inputs may be any that keep to these rules, and one draw needn't show every extreme that they name: `queries`: large in the hidden draw where a query row copies its own key. `dest_group`: the 2 documents of a device go to two different groups, never its own; document k of every device of one fsdp index moves the same number of groups ahead. `source_group`: consistent with dest_group: every device receives exactly one document for each of its slots, at most one from each sender.
All inputs are finite; a program needn't handle non-finite values.
Results may differ from the reference program's by a relative error of at most 0.0075.
Values may be sent and summed in bfloat16 or wider, within the bound.
No kernel may reach another device: no remote copies, remote signals or barrier semaphores. Data moves between devices by JAX's collectives and lax.ppermute only.
A program may use at most 128 MiB of HBM per device.

```python
import jax
import jax.numpy as jnp
from jax import lax

D = 8192
HEADS = 32
KV_HEADS = 4
HEAD_DIM = 128
SEG = 64
MEM = 64
SLOTS = 2
KVW = 512
QW = 4096
N_FSDP = 64
N_DP = 4


def key_draw(key):
    array_shape = (N_DP, N_FSDP * SLOTS * SEG, KV_HEADS * HEAD_DIM)
    normal_part = jax.random.normal(jax.random.fold_in(key, 11), array_shape, jnp.float32)
    return jnp.clip(normal_part, -4.0, 4.0)


def draw_keys(key, part):
    return key_draw(key).astype(jnp.bfloat16)


def draw_queries(key, part):
    row_total = N_FSDP * SLOTS * SEG
    array_shape = (N_DP, row_total, HEADS * HEAD_DIM)
    normal_part = jnp.clip(jax.random.normal(jax.random.fold_in(key, 21), array_shape, jnp.float32), -4.0, 4.0)
    return normal_part.astype(jnp.bfloat16)


def shift_table(key):
    first_shift = jax.random.randint(jax.random.fold_in(key, 5), (N_FSDP,), 1, N_DP)
    offset = jax.random.randint(jax.random.fold_in(key, 6), (N_FSDP,), 1, N_DP - 1)
    second_shift = 1 + (first_shift - 1 + offset) % (N_DP - 1)
    return jnp.stack([first_shift, second_shift], axis=1).astype(jnp.int32)


def draw_dest_group(key, part):
    shifts = shift_table(key)
    groups = jnp.arange(N_DP, dtype=jnp.int32)[:, None, None]
    return ((groups + shifts[None]) % N_DP).reshape(N_DP, N_FSDP * SLOTS).astype(jnp.int32)


def draw_source_group(key, part):
    shifts = shift_table(key)
    groups = jnp.arange(N_DP, dtype=jnp.int32)[:, None, None]
    return ((groups - shifts[None] + N_DP) % N_DP).reshape(N_DP, N_FSDP * SLOTS).astype(jnp.int32)


def plant(result, stream_key, least, largest):
    index_at = [jax.random.randint(jax.random.fold_in(stream_key, axis), (), 0, length) for axis, length in enumerate(result.shape)]
    main_axis = result.shape.index(max(result.shape))
    beside = index_at[:main_axis] + [(index_at[main_axis] + 1) % result.shape[main_axis]] + index_at[main_axis + 1:]
    return result.at[tuple(index_at)].set(least).at[tuple(beside)].set(largest)


def level_of(own_key, dims, split, low, largest):
    def one(dim, blocks):
        heights = jax.random.uniform(jax.random.fold_in(jax.random.fold_in(own_key, 6), dim), (blocks,), jnp.float32, low / len(split), largest / len(split))
        return jnp.repeat(jnp.exp(heights), dims[dim] // blocks).reshape((-1,) + (1,) * (len(dims) - dim - 1))

    level = one(*split[0])
    for cut in split[1:]:
        level = level * one(*cut)
    return level


def gaussian(key, shape, scale, bound, split=(), kind=jnp.bfloat16):
    entries = scale * jax.random.normal(key, shape, jnp.float32)
    if split:
        entries = entries * level_of(key, shape, split, -0.22, 0.18)
    return jnp.clip(entries, -bound, bound).astype(kind)


def setup_inputs(seed: int = 0) -> dict:
    seeds = jax.random.split(jax.random.key(seed), 11)
    tokens = gaussian(seeds[0], (N_DP, N_FSDP * SLOTS * SEG, D), 1.0, 6.0, ((0, 4), (1, 64)))
    queries = draw_queries(jax.random.fold_in(seeds[10], 71), 0)
    keys = draw_keys(jax.random.fold_in(seeds[10], 71), 0)
    memory = gaussian(seeds[3], (N_DP, N_FSDP * SLOTS * MEM, D), 1.0, 6.0, ((0, 4), (1, 64)))
    mem_keys = gaussian(seeds[4], (N_DP, N_FSDP * SLOTS * MEM, KVW), 1.0, 4.0, ((0, 4), (1, 64)))
    cotangent = gaussian(seeds[5], (N_DP, N_FSDP * SLOTS * SEG, QW), 1.0, 6.0, ((0, 4), (1, 64)))
    value_weight = gaussian(seeds[6], (D, KVW), D ** -0.5, 0.0625, ((0, 64),))
    dest_group = draw_dest_group(jax.random.fold_in(seeds[10], 71), 0)
    source_group = draw_source_group(jax.random.fold_in(seeds[10], 71), 0)
    lengths = plant(jax.random.randint(seeds[9], (N_DP, N_FSDP * SLOTS), 1, SEG + 1), jax.random.fold_in(seeds[9], 1), 1, SEG).astype(jnp.int32)
    return {"tokens": tokens, "queries": queries, "keys": keys, "memory": memory, "mem_keys": mem_keys, "cotangent": cotangent, "value_weight": value_weight, "dest_group": dest_group, "source_group": source_group, "lengths": lengths}


def round_low(array):
    return lax.optimization_barrier(array.astype(jnp.bfloat16)).astype(jnp.float32)


def attend(query_rows, seg_keys, seg_values, slot_keys, slot_values, upstream, length):
    seg_len = query_rows.shape[0]
    mem_len = slot_keys.shape[0]
    kv_width = seg_keys.shape[1]
    heads_kv = kv_width // HEAD_DIM
    group_size = query_rows.shape[1] // kv_width
    key_count = seg_len + mem_len
    all_keys = jnp.concatenate([slot_keys, seg_keys], axis=0).astype(jnp.float32).reshape(key_count, heads_kv, HEAD_DIM)
    all_values = jnp.concatenate([slot_values, seg_values], axis=0).astype(jnp.float32).reshape(key_count, heads_kv, HEAD_DIM)
    query_heads = query_rows.astype(jnp.float32).reshape(seg_len, heads_kv, group_size, HEAD_DIM)
    score_scale = HEAD_DIM ** -0.5
    scores = jnp.einsum("qkgd,jkd->kgqj", query_heads, all_keys) * score_scale
    positions = jnp.arange(seg_len)[:, None]
    columns = jnp.arange(key_count)[None, :]
    visible = (columns < mem_len) | (columns - mem_len <= positions)
    scores = jnp.where(visible, scores, -1e30)
    row_max = jnp.max(scores, axis=-1, keepdims=True)
    exp_scores = jnp.exp(scores - row_max)
    weights = exp_scores / jnp.sum(exp_scores, axis=-1, keepdims=True)
    weights_low = round_low(weights)
    output = round_low(jnp.einsum("kgqj,jkd->qkgd", weights_low, all_values))
    live_rows = (jnp.arange(seg_len) < length).astype(jnp.float32)
    masked = upstream.astype(jnp.float32).reshape(seg_len, heads_kv, group_size, HEAD_DIM) * live_rows[:, None, None, None]
    grad_weights = jnp.einsum("qkgd,jkd->kgqj", masked, all_values)
    grad_values = jnp.einsum("kgqj,qkgd->jkd", weights_low, masked).reshape(key_count, kv_width)
    row_delta = jnp.einsum("qkgd,qkgd->kgq", masked, output)
    grad_scores = round_low(weights * (grad_weights - row_delta[..., None]) * score_scale)
    grad_query = jnp.einsum("kgqj,jkd->qkgd", grad_scores, all_keys).reshape(seg_len, -1).astype(jnp.bfloat16)
    grad_all_keys = jnp.einsum("kgqj,qkgd->jkd", grad_scores, query_heads).reshape(key_count, kv_width)
    return grad_query, grad_all_keys[:mem_len], grad_all_keys[mem_len:], grad_values[:mem_len], grad_values[mem_len:]


def reference(tokens, queries, keys, memory, mem_keys, cotangent, value_weight, dest_group, source_group, lengths):
    kv_width = KV_HEADS * HEAD_DIM
    q_width = HEADS * HEAD_DIM
    token_flat = tokens.reshape(-1, D)
    memory_flat = memory.reshape(-1, D)
    seg_values = jnp.dot(token_flat, value_weight, preferred_element_type=jnp.float32).astype(jnp.bfloat16)
    mem_values = jnp.dot(memory_flat, value_weight, preferred_element_type=jnp.float32).astype(jnp.bfloat16)
    doc_shape = (N_DP, N_FSDP, SLOTS, MEM, kv_width)
    source_index = jnp.broadcast_to(source_group.reshape(N_DP, N_FSDP, SLOTS, 1, 1), doc_shape).astype(jnp.int32)
    slot_keys = jnp.take_along_axis(mem_keys.reshape(doc_shape), source_index, axis=0)
    slot_values = jnp.take_along_axis(mem_values.reshape(doc_shape), source_index, axis=0)
    blocks = N_DP * N_FSDP
    inputs = (queries.reshape(blocks, SLOTS, SEG, q_width),
              keys.reshape(blocks, SLOTS, SEG, kv_width),
              seg_values.reshape(blocks, SLOTS, SEG, kv_width),
              slot_keys.reshape(blocks, SLOTS, MEM, kv_width),
              slot_values.reshape(blocks, SLOTS, MEM, kv_width),
              cotangent.reshape(blocks, SLOTS, SEG, q_width),
              lengths.reshape(blocks, SLOTS))

    def one_block(pieces):
        return jax.vmap(attend)(*pieces)

    grad_query, slot_grad_keys, seg_grad_keys, slot_grad_values, seg_grad_values = lax.map(one_block, inputs)
    dest_index = jnp.broadcast_to(dest_group.reshape(N_DP, N_FSDP, SLOTS, 1, 1), doc_shape).astype(jnp.int32)
    back_keys = slot_grad_keys.astype(jnp.bfloat16).reshape(doc_shape)
    back_values = slot_grad_values.astype(jnp.bfloat16).reshape(doc_shape)
    doc_grad_keys = jnp.take_along_axis(back_keys, dest_index, axis=0)
    doc_grad_values = jnp.take_along_axis(back_values, dest_index, axis=0).reshape(-1, kv_width)
    grad_memory = jnp.dot(doc_grad_values, value_weight.T, preferred_element_type=jnp.float32).astype(jnp.bfloat16)
    seg_low = seg_grad_values.astype(jnp.bfloat16).reshape(-1, kv_width)
    grad_weight = jnp.dot(token_flat.T, seg_low, preferred_element_type=jnp.float32) + jnp.dot(memory_flat.T, doc_grad_values, preferred_element_type=jnp.float32)
    return (grad_query.reshape(N_DP, N_FSDP * SLOTS * SEG, q_width),
            seg_grad_keys.astype(jnp.bfloat16).reshape(N_DP, N_FSDP * SLOTS * SEG, kv_width),
            grad_memory.reshape(N_DP, N_FSDP * SLOTS * MEM, D),
            doc_grad_keys.reshape(N_DP, N_FSDP * SLOTS * MEM, kv_width),
            grad_weight.astype(jnp.bfloat16))
```

```python
import jax
import jax.numpy as jnp
from jax import lax
from jax.sharding import Mesh, PartitionSpec as P

HEAD_DIM = 128


def attend(query_rows, seg_keys, seg_values, slot_keys, slot_values, upstream, length):
    seg_len = query_rows.shape[0]
    mem_len = slot_keys.shape[0]
    kv_width = seg_keys.shape[1]
    heads_kv = kv_width // HEAD_DIM
    group_size = query_rows.shape[1] // kv_width
    key_count = seg_len + mem_len
    all_keys = jnp.concatenate([slot_keys, seg_keys], axis=0).reshape(key_count, heads_kv, HEAD_DIM)
    all_values = jnp.concatenate([slot_values, seg_values], axis=0).reshape(
        key_count, heads_kv, HEAD_DIM
    )
    query_heads = query_rows.reshape(seg_len, heads_kv, group_size, HEAD_DIM)
    score_scale = HEAD_DIM ** (-0.5)
    scores = (
        jnp.einsum("qkgd,jkd->kgqj", query_heads, all_keys, preferred_element_type=jnp.float32)
        * score_scale
    )
    positions = jnp.arange(seg_len)[:, None]
    columns = jnp.arange(key_count)[None, :]
    visible = (columns < mem_len) | (columns - mem_len <= positions)
    scores = jnp.where(visible, scores, -1e30)
    row_max = jnp.max(scores, axis=-1, keepdims=True)
    exp_scores = jnp.exp(scores - row_max)
    weights = exp_scores / jnp.sum(exp_scores, axis=-1, keepdims=True)
    weights_low = weights.astype(jnp.bfloat16)
    output = jnp.einsum(
        "kgqj,jkd->qkgd", weights_low, all_values, preferred_element_type=jnp.float32
    ).astype(jnp.bfloat16)
    live_rows = (jnp.arange(seg_len) < length).astype(jnp.bfloat16)
    masked = (
        upstream.reshape(seg_len, heads_kv, group_size, HEAD_DIM) * live_rows[:, None, None, None]
    )
    grad_weights = jnp.einsum(
        "qkgd,jkd->kgqj", masked, all_values, preferred_element_type=jnp.float32
    )
    grad_values = jnp.einsum(
        "kgqj,qkgd->jkd", weights_low, masked, preferred_element_type=jnp.float32
    ).reshape(key_count, kv_width)
    row_delta = jnp.einsum("qkgd,qkgd->kgq", masked, output, preferred_element_type=jnp.float32)
    grad_scores = (weights * (grad_weights - row_delta[..., None]) * score_scale).astype(
        jnp.bfloat16
    )
    grad_query = (
        jnp.einsum("kgqj,jkd->qkgd", grad_scores, all_keys, preferred_element_type=jnp.float32)
        .reshape(seg_len, -1)
        .astype(jnp.bfloat16)
    )
    grad_all_keys = jnp.einsum(
        "kgqj,qkgd->jkd", grad_scores, query_heads, preferred_element_type=jnp.float32
    ).reshape(key_count, kv_width)
    return (
        grad_query,
        grad_all_keys[:mem_len],
        grad_all_keys[mem_len:],
        grad_values[:mem_len],
        grad_values[mem_len:],
    )


FSDP_AXES = ("fx", "fz", "fy")
DP_AXES = ("dx", "dc")


def to_block_order(cols, split):
    fx, fz, fy = split
    rows = cols.shape[0]
    block = cols.shape[1] // (fx * fz * fy)
    return cols.reshape(rows, fx, fz, fy, block).transpose(0, 2, 3, 1, 4).reshape(rows, -1)


def from_block_order(cols, split):
    fx, fz, fy = split
    rows = cols.shape[0]
    block = cols.shape[1] // (fx * fz * fy)
    return cols.reshape(rows, fz, fy, fx, block).transpose(0, 3, 1, 2, 4).reshape(rows, -1)


def per_device(
    tokens,
    queries,
    keys,
    memory,
    mem_keys,
    cotangent,
    value_weight,
    dest_group,
    source_group,
    lengths,
):
    split = tuple(lax.axis_size(a) for a in FSDP_AXES)
    cores = lax.axis_size("dc")
    groups = lax.axis_size("dx") * cores
    slot_count = dest_group.shape[1]
    seg_len = tokens.shape[1] // slot_count
    mem_len = memory.shape[1] // slot_count
    kv_width = value_weight.shape[1]
    model_width = tokens.shape[2]
    half = kv_width // cores
    core = lax.axis_index("dc")
    part = lax.dynamic_slice_in_dim(value_weight, core * half, half, axis=1)
    part = lax.all_gather(part, "fx", axis=0, tiled=True)
    part = lax.all_gather(part, "fy", axis=0, tiled=True)
    part = lax.all_gather(part, "fz", axis=0, tiled=True)
    weight_full = lax.all_gather(part, "dc", axis=1, tiled=True)
    stacked = to_block_order(jnp.concatenate([tokens[0], memory[0]], axis=0), split)
    values = jnp.dot(stacked, weight_full, preferred_element_type=jnp.float32).astype(jnp.bfloat16)
    split_at = slot_count * seg_len
    seg_values = values[:split_at].reshape(slot_count, seg_len, kv_width)
    doc_values = values[split_at:].reshape(slot_count, mem_len, kv_width)
    doc_keys = mem_keys[0].reshape(slot_count, mem_len, kv_width)
    targets = jnp.arange(groups, dtype=jnp.int32)
    send_table = (dest_group[0][None, :] == targets[:, None]).astype(jnp.bfloat16)
    take_table = (source_group[0][:, None] == targets[None, :]).astype(jnp.bfloat16)
    out_keys = jnp.einsum(
        "hs,smc->hmc", send_table, doc_keys, preferred_element_type=jnp.float32
    ).astype(jnp.bfloat16)
    out_values = jnp.einsum(
        "hs,smc->hmc", send_table, doc_values, preferred_element_type=jnp.float32
    ).astype(jnp.bfloat16)
    in_keys, in_values = (
        lax.all_to_all(out_keys, DP_AXES, split_axis=0, concat_axis=0, tiled=True),
        lax.all_to_all(out_values, DP_AXES, split_axis=0, concat_axis=0, tiled=True),
    )
    slot_keys = jnp.einsum(
        "sh,hmc->smc", take_table, in_keys, preferred_element_type=jnp.float32
    ).astype(jnp.bfloat16)
    slot_values = jnp.einsum(
        "sh,hmc->smc", take_table, in_values, preferred_element_type=jnp.float32
    ).astype(jnp.bfloat16)
    query_slots = queries[0].reshape(slot_count, seg_len, -1)
    key_slots = keys[0].reshape(slot_count, seg_len, kv_width)
    upstream_slots = cotangent[0].reshape(slot_count, seg_len, -1)
    grad_query, slot_grad_keys, seg_grad_keys, slot_grad_values, seg_grad_values = jax.vmap(attend)(
        query_slots, key_slots, seg_values, slot_keys, slot_values, upstream_slots, lengths[0]
    )
    back_keys = jnp.einsum(
        "sh,smc->hmc",
        take_table,
        slot_grad_keys.astype(jnp.bfloat16),
        preferred_element_type=jnp.float32,
    ).astype(jnp.bfloat16)
    back_values = jnp.einsum(
        "sh,smc->hmc",
        take_table,
        slot_grad_values.astype(jnp.bfloat16),
        preferred_element_type=jnp.float32,
    ).astype(jnp.bfloat16)
    ret_keys, ret_values = (
        lax.all_to_all(back_keys, DP_AXES, split_axis=0, concat_axis=0, tiled=True),
        lax.all_to_all(back_values, DP_AXES, split_axis=0, concat_axis=0, tiled=True),
    )
    doc_grad_keys = jnp.einsum(
        "hs,hmc->smc", send_table, ret_keys, preferred_element_type=jnp.float32
    ).astype(jnp.bfloat16)
    doc_grad_values = jnp.einsum(
        "hs,hmc->smc", send_table, ret_values, preferred_element_type=jnp.float32
    ).astype(jnp.bfloat16)
    doc_grad_flat = doc_grad_values.reshape(slot_count * mem_len, kv_width)
    grad_memory = from_block_order(
        lax.dot_general(
            doc_grad_flat, weight_full, (((1,), (1,)), ((), ())), preferred_element_type=jnp.float32
        ).astype(jnp.bfloat16),
        split,
    )
    value_grads_all = jnp.concatenate(
        [seg_grad_values.astype(jnp.bfloat16).reshape(-1, kv_width), doc_grad_flat], axis=0
    )
    partial = lax.dot_general(
        stacked, value_grads_all, (((0,), (0,)), ((), ())), preferred_element_type=jnp.float32
    )
    shares = lax.psum_scatter(partial, "dc", scatter_dimension=1, tiled=True)
    shares = lax.psum_scatter(shares, "fz", scatter_dimension=0, tiled=True)
    shares = lax.psum_scatter(shares, "fy", scatter_dimension=0, tiled=True)
    shares = lax.psum_scatter(shares, "fx", scatter_dimension=0, tiled=True)
    shares = lax.psum(shares, "dx")
    grad_weight = lax.all_gather(shares, "dc", axis=1, tiled=True).astype(jnp.bfloat16)
    return (
        grad_query.reshape(1, slot_count * seg_len, -1),
        seg_grad_keys.astype(jnp.bfloat16).reshape(1, slot_count * seg_len, kv_width),
        grad_memory.reshape(1, slot_count * mem_len, model_width),
        doc_grad_keys.reshape(1, slot_count * mem_len, kv_width),
        grad_weight,
    )


def refined_mesh(mesh):
    fsdp, dp = mesh.shape["fsdp"], mesh.shape["dp"]
    devices = mesh.devices.reshape(2, fsdp // 2 // 4, 4, 2, dp // 2)
    return Mesh(devices, FSDP_AXES + DP_AXES)


def solution(mesh):
    fine = refined_mesh(mesh)
    row = P(DP_AXES, FSDP_AXES, None)
    table = P(DP_AXES, FSDP_AXES)
    in_specs = (row, row, row, row, row, row, P(FSDP_AXES, None), table, table, table)
    out_specs = (row, row, row, row, P(FSDP_AXES, None))
    return jax.shard_map(
        per_device, mesh=fine, in_specs=in_specs, out_specs=out_specs, check_vma=False
    )
```

```python
import jax
import jax.numpy as jnp
from jax import lax
from jax.sharding import Mesh, PartitionSpec as P

HEAD_DIM = 128


def attend(query_rows, seg_keys, seg_values, slot_keys, slot_values, upstream, length):
    seg_len = query_rows.shape[0]
    mem_len = slot_keys.shape[0]
    kv_width = seg_keys.shape[1]
    heads_kv = kv_width // HEAD_DIM
    group_size = query_rows.shape[1] // kv_width
    key_count = seg_len + mem_len
    all_keys = jnp.concatenate([slot_keys, seg_keys], axis=0).reshape(key_count, heads_kv, HEAD_DIM)
    all_values = jnp.concatenate([slot_values, seg_values], axis=0).reshape(
        key_count, heads_kv, HEAD_DIM
    )
    query_heads = query_rows.reshape(seg_len, heads_kv, group_size, HEAD_DIM)
    score_scale = HEAD_DIM ** (-0.5)
    scores = (
        jnp.einsum("qkgd,jkd->kgqj", query_heads, all_keys, preferred_element_type=jnp.float32)
        * score_scale
    )
    positions = jnp.arange(seg_len)[:, None]
    columns = jnp.arange(key_count)[None, :]
    visible = (columns < mem_len) | (columns - mem_len <= positions)
    scores = jnp.where(visible, scores, -1e30)
    row_max = jnp.max(scores, axis=-1, keepdims=True)
    exp_scores = jnp.exp(scores - row_max)
    weights = exp_scores / jnp.sum(exp_scores, axis=-1, keepdims=True)
    weights_low = weights.astype(jnp.bfloat16)
    output = jnp.einsum(
        "kgqj,jkd->qkgd", weights_low, all_values, preferred_element_type=jnp.float32
    ).astype(jnp.bfloat16)
    live_rows = (jnp.arange(seg_len) < length).astype(jnp.bfloat16)
    masked = (
        upstream.reshape(seg_len, heads_kv, group_size, HEAD_DIM) * live_rows[:, None, None, None]
    )
    grad_weights = jnp.einsum(
        "qkgd,jkd->kgqj", masked, all_values, preferred_element_type=jnp.float32
    )
    grad_values = jnp.einsum(
        "kgqj,qkgd->jkd", weights_low, masked, preferred_element_type=jnp.float32
    ).reshape(key_count, kv_width)
    row_delta = jnp.einsum("qkgd,qkgd->kgq", masked, output, preferred_element_type=jnp.float32)
    grad_scores = (weights * (grad_weights - row_delta[..., None]) * score_scale).astype(
        jnp.bfloat16
    )
    grad_query = (
        jnp.einsum("kgqj,jkd->qkgd", grad_scores, all_keys, preferred_element_type=jnp.float32)
        .reshape(seg_len, -1)
        .astype(jnp.bfloat16)
    )
    grad_all_keys = jnp.einsum(
        "kgqj,qkgd->jkd", grad_scores, query_heads, preferred_element_type=jnp.float32
    ).reshape(key_count, kv_width)
    return (
        grad_query,
        grad_all_keys[:mem_len],
        grad_all_keys[mem_len:],
        grad_values[:mem_len],
        grad_values[mem_len:],
    )


FSDP_AXES = ("fx", "fz", "fy")
DP_AXES = ("dx", "dc")


def to_block_order(cols, split):
    fx, fz, fy = split
    rows = cols.shape[0]
    block = cols.shape[1] // (fx * fz * fy)
    return cols.reshape(rows, fx, fz, fy, block).transpose(0, 2, 3, 1, 4).reshape(rows, -1)


def from_block_order(cols, split):
    fx, fz, fy = split
    rows = cols.shape[0]
    block = cols.shape[1] // (fx * fz * fy)
    return cols.reshape(rows, fz, fy, fx, block).transpose(0, 3, 1, 2, 4).reshape(rows, -1)


def per_device(
    tokens,
    queries,
    keys,
    memory,
    mem_keys,
    cotangent,
    value_weight,
    dest_group,
    source_group,
    lengths,
):
    split = tuple(lax.axis_size(a) for a in FSDP_AXES)
    cores = lax.axis_size("dc")
    groups = lax.axis_size("dx") * cores
    slot_count = dest_group.shape[1]
    seg_len = tokens.shape[1] // slot_count
    mem_len = memory.shape[1] // slot_count
    kv_width = value_weight.shape[1]
    model_width = tokens.shape[2]
    half = kv_width // cores
    core = lax.axis_index("dc")
    part = lax.dynamic_slice_in_dim(value_weight, core * half, half, axis=1)
    part = lax.all_gather(part, "fx", axis=0, tiled=True)
    part = lax.all_gather(part, "fy", axis=0, tiled=True)
    part = lax.all_gather(part, "fz", axis=0, tiled=True)
    weight_full = lax.all_gather(part, "dc", axis=1, tiled=True)
    stacked = to_block_order(jnp.concatenate([tokens[0], memory[0]], axis=0), split)
    values = jnp.dot(stacked, weight_full, preferred_element_type=jnp.float32).astype(jnp.bfloat16)
    split_at = slot_count * seg_len
    seg_values = values[:split_at].reshape(slot_count, seg_len, kv_width)
    doc_values = values[split_at:].reshape(slot_count, mem_len, kv_width)
    doc_keys = mem_keys[0].reshape(slot_count, mem_len, kv_width)
    targets = jnp.arange(groups, dtype=jnp.int32)
    send_table = (dest_group[0][None, :] == targets[:, None]).astype(jnp.bfloat16)
    take_table = (source_group[0][:, None] == targets[None, :]).astype(jnp.bfloat16)
    out_keys = jnp.einsum(
        "hs,smc->hmc", send_table, doc_keys, preferred_element_type=jnp.float32
    ).astype(jnp.bfloat16)
    out_values = jnp.einsum(
        "hs,smc->hmc", send_table, doc_values, preferred_element_type=jnp.float32
    ).astype(jnp.bfloat16)
    in_keys, in_values = (
        lax.all_to_all(out_keys, DP_AXES, split_axis=0, concat_axis=0, tiled=True),
        lax.all_to_all(out_values, DP_AXES, split_axis=0, concat_axis=0, tiled=True),
    )
    slot_keys = jnp.einsum(
        "sh,hmc->smc", take_table, in_keys, preferred_element_type=jnp.float32
    ).astype(jnp.bfloat16)
    slot_values = jnp.einsum(
        "sh,hmc->smc", take_table, in_values, preferred_element_type=jnp.float32
    ).astype(jnp.bfloat16)
    query_slots = queries[0].reshape(slot_count, seg_len, -1)
    key_slots = keys[0].reshape(slot_count, seg_len, kv_width)
    upstream_slots = cotangent[0].reshape(slot_count, seg_len, -1)
    grad_query, slot_grad_keys, seg_grad_keys, slot_grad_values, seg_grad_values = jax.vmap(attend)(
        query_slots, key_slots, seg_values, slot_keys, slot_values, upstream_slots, lengths[0]
    )
    back_keys = jnp.einsum(
        "sh,smc->hmc",
        take_table,
        slot_grad_keys.astype(jnp.bfloat16),
        preferred_element_type=jnp.float32,
    ).astype(jnp.bfloat16)
    back_values = jnp.einsum(
        "sh,smc->hmc",
        take_table,
        slot_grad_values.astype(jnp.bfloat16),
        preferred_element_type=jnp.float32,
    ).astype(jnp.bfloat16)
    ret_keys, ret_values = (
        lax.all_to_all(back_keys, DP_AXES, split_axis=0, concat_axis=0, tiled=True),
        lax.all_to_all(back_values, DP_AXES, split_axis=0, concat_axis=0, tiled=True),
    )
    doc_grad_keys = jnp.einsum(
        "hs,hmc->smc", send_table, ret_keys, preferred_element_type=jnp.float32
    ).astype(jnp.bfloat16)
    doc_grad_values = jnp.einsum(
        "hs,hmc->smc", send_table, ret_values, preferred_element_type=jnp.float32
    ).astype(jnp.bfloat16)
    doc_grad_flat = doc_grad_values.reshape(slot_count * mem_len, kv_width)
    grad_memory = from_block_order(
        lax.dot_general(
            doc_grad_flat, weight_full, (((1,), (1,)), ((), ())), preferred_element_type=jnp.float32
        ).astype(jnp.bfloat16),
        split,
    )
    value_grads_all = jnp.concatenate(
        [seg_grad_values.astype(jnp.bfloat16).reshape(-1, kv_width), doc_grad_flat], axis=0
    )
    partial = lax.dot_general(
        stacked, value_grads_all, (((0,), (0,)), ((), ())), preferred_element_type=jnp.float32
    )
    shares = lax.psum_scatter(partial.astype(jnp.bfloat16), "dc", scatter_dimension=1, tiled=True)
    shares = lax.psum_scatter(shares, "fz", scatter_dimension=0, tiled=True)
    shares = lax.psum_scatter(shares, "fy", scatter_dimension=0, tiled=True)
    shares = lax.psum_scatter(shares, "fx", scatter_dimension=0, tiled=True)
    shares = lax.psum(shares, "dx")
    grad_weight = lax.all_gather(shares, "dc", axis=1, tiled=True).astype(jnp.bfloat16)
    return (
        grad_query.reshape(1, slot_count * seg_len, -1),
        seg_grad_keys.astype(jnp.bfloat16).reshape(1, slot_count * seg_len, kv_width),
        grad_memory.reshape(1, slot_count * mem_len, model_width),
        doc_grad_keys.reshape(1, slot_count * mem_len, kv_width),
        grad_weight,
    )


def refined_mesh(mesh):
    fsdp, dp = mesh.shape["fsdp"], mesh.shape["dp"]
    devices = mesh.devices.reshape(2, fsdp // 2 // 4, 4, 2, dp // 2)
    return Mesh(devices, FSDP_AXES + DP_AXES)


def solution(mesh):
    fine = refined_mesh(mesh)
    row = P(DP_AXES, FSDP_AXES, None)
    table = P(DP_AXES, FSDP_AXES)
    in_specs = (row, row, row, row, row, row, P(FSDP_AXES, None), table, table, table)
    out_specs = (row, row, row, row, P(FSDP_AXES, None))
    return jax.shard_map(
        per_device, mesh=fine, in_specs=in_specs, out_specs=out_specs, check_vma=False
    )
```

```python
import jax
import jax.numpy as jnp
from jax import lax
from jax.sharding import Mesh, PartitionSpec as P

HEAD_DIM = 128


def attend(query_rows, seg_keys, seg_values, slot_keys, slot_values, upstream, length):
    seg_len = query_rows.shape[0]
    mem_len = slot_keys.shape[0]
    kv_width = seg_keys.shape[1]
    heads_kv = kv_width // HEAD_DIM
    group_size = query_rows.shape[1] // kv_width
    key_count = seg_len + mem_len
    all_keys = jnp.concatenate([slot_keys, seg_keys], axis=0).reshape(key_count, heads_kv, HEAD_DIM)
    all_values = jnp.concatenate([slot_values, seg_values], axis=0).reshape(
        key_count, heads_kv, HEAD_DIM
    )
    query_heads = query_rows.reshape(seg_len, heads_kv, group_size, HEAD_DIM)
    score_scale = HEAD_DIM ** (-0.5)
    scores = (
        jnp.einsum("qkgd,jkd->kgqj", query_heads, all_keys, preferred_element_type=jnp.float32)
        * score_scale
    )
    positions = jnp.arange(seg_len)[:, None]
    columns = jnp.arange(key_count)[None, :]
    visible = (columns < mem_len) | (columns - mem_len <= positions)
    scores = jnp.where(visible, scores, -1e30)
    row_max = jnp.max(scores, axis=-1, keepdims=True)
    exp_scores = jnp.exp(scores - row_max)
    weights = exp_scores / jnp.sum(exp_scores, axis=-1, keepdims=True)
    weights_low = weights.astype(jnp.bfloat16)
    output = jnp.einsum(
        "kgqj,jkd->qkgd", weights_low, all_values, preferred_element_type=jnp.float32
    ).astype(jnp.bfloat16)
    live_rows = (jnp.arange(seg_len) < length).astype(jnp.bfloat16)
    masked = (
        upstream.reshape(seg_len, heads_kv, group_size, HEAD_DIM) * live_rows[:, None, None, None]
    )
    grad_weights = jnp.einsum(
        "qkgd,jkd->kgqj", masked, all_values, preferred_element_type=jnp.float32
    )
    grad_values = jnp.einsum(
        "kgqj,qkgd->jkd", weights_low, masked, preferred_element_type=jnp.float32
    ).reshape(key_count, kv_width)
    row_delta = jnp.einsum("qkgd,qkgd->kgq", masked, output, preferred_element_type=jnp.float32)
    grad_scores = (weights * (grad_weights - row_delta[..., None]) * score_scale).astype(
        jnp.bfloat16
    )
    grad_query = (
        jnp.einsum("kgqj,jkd->qkgd", grad_scores, all_keys, preferred_element_type=jnp.float32)
        .reshape(seg_len, -1)
        .astype(jnp.bfloat16)
    )
    grad_all_keys = jnp.einsum(
        "kgqj,qkgd->jkd", grad_scores, query_heads, preferred_element_type=jnp.float32
    ).reshape(key_count, kv_width)
    return (
        grad_query,
        grad_all_keys[:mem_len],
        grad_all_keys[mem_len:],
        grad_values[:mem_len],
        grad_values[mem_len:],
    )


FSDP_AXES = ("fx", "fz", "fy")
DP_AXES = ("dx", "dc")


def to_block_order(cols, split):
    fx, fz, fy = split
    rows = cols.shape[0]
    block = cols.shape[1] // (fx * fz * fy)
    return cols.reshape(rows, fx, fz, fy, block).transpose(0, 2, 3, 1, 4).reshape(rows, -1)


def from_block_order(cols, split):
    fx, fz, fy = split
    rows = cols.shape[0]
    block = cols.shape[1] // (fx * fz * fy)
    return cols.reshape(rows, fz, fy, fx, block).transpose(0, 3, 1, 2, 4).reshape(rows, -1)


def per_device(
    tokens,
    queries,
    keys,
    memory,
    mem_keys,
    cotangent,
    value_weight,
    dest_group,
    source_group,
    lengths,
):
    split = tuple(lax.axis_size(a) for a in FSDP_AXES)
    cores = lax.axis_size("dc")
    groups = lax.axis_size("dx") * cores
    slot_count = dest_group.shape[1]
    seg_len = tokens.shape[1] // slot_count
    mem_len = memory.shape[1] // slot_count
    kv_width = value_weight.shape[1]
    model_width = tokens.shape[2]
    half = kv_width // cores
    core = lax.axis_index("dc")
    part = lax.dynamic_slice_in_dim(value_weight, core * half, half, axis=1)
    part = lax.all_gather(part, "fx", axis=0, tiled=True)
    part = lax.all_gather(part, "fy", axis=0, tiled=True)
    part = lax.all_gather(part, "fz", axis=0, tiled=True)
    weight_full = lax.all_gather(part, "dc", axis=1, tiled=True)
    stacked = to_block_order(jnp.concatenate([tokens[0], memory[0]], axis=0), split)
    partner_stacked = lax.ppermute(stacked, "dc", [(c, (c + 1) % cores) for c in range(cores)])
    values = jnp.dot(stacked, weight_full, preferred_element_type=jnp.float32).astype(jnp.bfloat16)
    split_at = slot_count * seg_len
    seg_values = values[:split_at].reshape(slot_count, seg_len, kv_width)
    doc_values = values[split_at:].reshape(slot_count, mem_len, kv_width)
    doc_keys = mem_keys[0].reshape(slot_count, mem_len, kv_width)
    targets = jnp.arange(groups, dtype=jnp.int32)
    send_table = (dest_group[0][None, :] == targets[:, None]).astype(jnp.bfloat16)
    take_table = (source_group[0][:, None] == targets[None, :]).astype(jnp.bfloat16)
    out_keys = jnp.einsum(
        "hs,smc->hmc", send_table, doc_keys, preferred_element_type=jnp.float32
    ).astype(jnp.bfloat16)
    out_values = jnp.einsum(
        "hs,smc->hmc", send_table, doc_values, preferred_element_type=jnp.float32
    ).astype(jnp.bfloat16)
    in_keys, in_values = (
        lax.all_to_all(out_keys, DP_AXES, split_axis=0, concat_axis=0, tiled=True),
        lax.all_to_all(out_values, DP_AXES, split_axis=0, concat_axis=0, tiled=True),
    )
    slot_keys = jnp.einsum(
        "sh,hmc->smc", take_table, in_keys, preferred_element_type=jnp.float32
    ).astype(jnp.bfloat16)
    slot_values = jnp.einsum(
        "sh,hmc->smc", take_table, in_values, preferred_element_type=jnp.float32
    ).astype(jnp.bfloat16)
    query_slots = queries[0].reshape(slot_count, seg_len, -1)
    key_slots = keys[0].reshape(slot_count, seg_len, kv_width)
    upstream_slots = cotangent[0].reshape(slot_count, seg_len, -1)
    grad_query, slot_grad_keys, seg_grad_keys, slot_grad_values, seg_grad_values = jax.vmap(attend)(
        query_slots, key_slots, seg_values, slot_keys, slot_values, upstream_slots, lengths[0]
    )
    back_keys = jnp.einsum(
        "sh,smc->hmc",
        take_table,
        slot_grad_keys.astype(jnp.bfloat16),
        preferred_element_type=jnp.float32,
    ).astype(jnp.bfloat16)
    back_values = jnp.einsum(
        "sh,smc->hmc",
        take_table,
        slot_grad_values.astype(jnp.bfloat16),
        preferred_element_type=jnp.float32,
    ).astype(jnp.bfloat16)
    ret_keys, ret_values = (
        lax.all_to_all(back_keys, DP_AXES, split_axis=0, concat_axis=0, tiled=True),
        lax.all_to_all(back_values, DP_AXES, split_axis=0, concat_axis=0, tiled=True),
    )
    doc_grad_keys = jnp.einsum(
        "hs,hmc->smc", send_table, ret_keys, preferred_element_type=jnp.float32
    ).astype(jnp.bfloat16)
    doc_grad_values = jnp.einsum(
        "hs,hmc->smc", send_table, ret_values, preferred_element_type=jnp.float32
    ).astype(jnp.bfloat16)
    doc_grad_flat = doc_grad_values.reshape(slot_count * mem_len, kv_width)
    grad_memory = from_block_order(
        lax.dot_general(
            doc_grad_flat, weight_full, (((1,), (1,)), ((), ())), preferred_element_type=jnp.float32
        ).astype(jnp.bfloat16),
        split,
    )
    value_grads_all = jnp.concatenate(
        [seg_grad_values.astype(jnp.bfloat16).reshape(-1, kv_width), doc_grad_flat], axis=0
    )
    grads_half = lax.dynamic_slice_in_dim(value_grads_all, core * half, half, axis=1)
    swap = [(c, (c + 1) % cores) for c in range(cores)]
    partner_grads = lax.ppermute(
        lax.dynamic_slice_in_dim(value_grads_all, (1 - core) * half, half, axis=1), "dc", swap
    )
    both_rows = jnp.concatenate([stacked, partner_stacked], axis=0)
    both_grads = jnp.concatenate([grads_half, partner_grads], axis=0)
    partial = lax.dot_general(
        both_rows, both_grads, (((0,), (0,)), ((), ())), preferred_element_type=jnp.float32
    )
    quarter = half // 2
    fx, fz, fy = split
    first = partial[:, :quarter]
    second = partial[:, quarter:].reshape(fz, fy, fx, -1, quarter).transpose(1, 0, 2, 3, 4)
    second = second.reshape(-1, quarter)
    first = lax.psum_scatter(first, "fz", scatter_dimension=0, tiled=True)
    second = lax.psum_scatter(second, "fy", scatter_dimension=0, tiled=True)
    first = lax.psum_scatter(first, "fy", scatter_dimension=0, tiled=True)
    second = lax.psum_scatter(second, "fz", scatter_dimension=0, tiled=True)
    first = lax.psum_scatter(first, "fx", scatter_dimension=0, tiled=True)
    second = lax.psum_scatter(second, "fx", scatter_dimension=0, tiled=True)
    shares = lax.psum(jnp.concatenate([first, second], axis=1), "dx")
    grad_weight = lax.all_gather(shares, "dc", axis=1, tiled=True).astype(jnp.bfloat16)
    return (
        grad_query.reshape(1, slot_count * seg_len, -1),
        seg_grad_keys.astype(jnp.bfloat16).reshape(1, slot_count * seg_len, kv_width),
        grad_memory.reshape(1, slot_count * mem_len, model_width),
        doc_grad_keys.reshape(1, slot_count * mem_len, kv_width),
        grad_weight,
    )


def refined_mesh(mesh):
    fsdp, dp = mesh.shape["fsdp"], mesh.shape["dp"]
    devices = mesh.devices.reshape(2, fsdp // 2 // 4, 4, 2, dp // 2)
    return Mesh(devices, FSDP_AXES + DP_AXES)


def solution(mesh):
    fine = refined_mesh(mesh)
    row = P(DP_AXES, FSDP_AXES, None)
    table = P(DP_AXES, FSDP_AXES)
    in_specs = (row, row, row, row, row, row, P(FSDP_AXES, None), table, table, table)
    out_specs = (row, row, row, row, P(FSDP_AXES, None))
    return jax.shard_map(
        per_device, mesh=fine, in_specs=in_specs, out_specs=out_specs, check_vma=False
    )
```

```python
import jax
import jax.numpy as jnp
from jax import lax
from jax.sharding import Mesh, PartitionSpec as P

HEAD_DIM = 128


def attend(query_rows, seg_keys, seg_values, slot_keys, slot_values, upstream, length):
    seg_len = query_rows.shape[0]
    mem_len = slot_keys.shape[0]
    kv_width = seg_keys.shape[1]
    heads_kv = kv_width // HEAD_DIM
    group_size = query_rows.shape[1] // kv_width
    key_count = seg_len + mem_len
    all_keys = jnp.concatenate([slot_keys, seg_keys], axis=0).reshape(key_count, heads_kv, HEAD_DIM)
    all_values = jnp.concatenate([slot_values, seg_values], axis=0).reshape(
        key_count, heads_kv, HEAD_DIM
    )
    query_heads = query_rows.reshape(seg_len, heads_kv, group_size, HEAD_DIM)
    score_scale = HEAD_DIM ** (-0.5)
    scores = (
        jnp.einsum("qkgd,jkd->kgqj", query_heads, all_keys, preferred_element_type=jnp.float32)
        * score_scale
    )
    positions = jnp.arange(seg_len)[:, None]
    columns = jnp.arange(key_count)[None, :]
    visible = (columns < mem_len) | (columns - mem_len <= positions)
    scores = jnp.where(visible, scores, -1e30)
    row_max = jnp.max(scores, axis=-1, keepdims=True)
    exp_scores = jnp.exp(scores - row_max)
    weights = exp_scores / jnp.sum(exp_scores, axis=-1, keepdims=True)
    weights_low = weights.astype(jnp.bfloat16)
    output = jnp.einsum(
        "kgqj,jkd->qkgd", weights_low, all_values, preferred_element_type=jnp.float32
    ).astype(jnp.bfloat16)
    live_rows = (jnp.arange(seg_len) < length).astype(jnp.bfloat16)
    masked = (
        upstream.reshape(seg_len, heads_kv, group_size, HEAD_DIM) * live_rows[:, None, None, None]
    )
    grad_weights = jnp.einsum(
        "qkgd,jkd->kgqj", masked, all_values, preferred_element_type=jnp.float32
    )
    grad_values = jnp.einsum(
        "kgqj,qkgd->jkd", weights_low, masked, preferred_element_type=jnp.float32
    ).reshape(key_count, kv_width)
    row_delta = jnp.einsum("qkgd,qkgd->kgq", masked, output, preferred_element_type=jnp.float32)
    grad_scores = (weights * (grad_weights - row_delta[..., None]) * score_scale).astype(
        jnp.bfloat16
    )
    grad_query = (
        jnp.einsum("kgqj,jkd->qkgd", grad_scores, all_keys, preferred_element_type=jnp.float32)
        .reshape(seg_len, -1)
        .astype(jnp.bfloat16)
    )
    grad_all_keys = jnp.einsum(
        "kgqj,qkgd->jkd", grad_scores, query_heads, preferred_element_type=jnp.float32
    ).reshape(key_count, kv_width)
    return (
        grad_query,
        grad_all_keys[:mem_len],
        grad_all_keys[mem_len:],
        grad_values[:mem_len],
        grad_values[mem_len:],
    )


FSDP_AXES = ("fx", "fz", "fy")
DP_AXES = ("dx", "dc")


def to_block_order(cols, split):
    fx, fz, fy = split
    rows = cols.shape[0]
    block = cols.shape[1] // (fx * fz * fy)
    return cols.reshape(rows, fx, fz, fy, block).transpose(0, 2, 3, 1, 4).reshape(rows, -1)


def from_block_order(cols, split):
    fx, fz, fy = split
    rows = cols.shape[0]
    block = cols.shape[1] // (fx * fz * fy)
    return cols.reshape(rows, fz, fy, fx, block).transpose(0, 3, 1, 2, 4).reshape(rows, -1)


def per_device(
    tokens,
    queries,
    keys,
    memory,
    mem_keys,
    cotangent,
    value_weight,
    dest_group,
    source_group,
    lengths,
):
    split = tuple(lax.axis_size(a) for a in FSDP_AXES)
    cores = lax.axis_size("dc")
    groups = lax.axis_size("dx") * cores
    slot_count = dest_group.shape[1]
    seg_len = tokens.shape[1] // slot_count
    mem_len = memory.shape[1] // slot_count
    kv_width = value_weight.shape[1]
    model_width = tokens.shape[2]
    half = kv_width // cores
    core = lax.axis_index("dc")
    part = lax.dynamic_slice_in_dim(value_weight, core * half, half, axis=1)
    part = lax.all_gather(part, "fx", axis=0, tiled=True)
    part = lax.all_gather(part, "fy", axis=0, tiled=True)
    part = lax.all_gather(part, "fz", axis=0, tiled=True)
    other = lax.ppermute(part, "dc", [(c, (c + 1) % cores) for c in range(cores)])
    pair = jnp.stack([part, other], axis=0)
    pair = jnp.where(core == 0, pair, pair[::-1])
    weight_full = jnp.concatenate([pair[0], pair[1]], axis=1)
    stacked = to_block_order(jnp.concatenate([tokens[0], memory[0]], axis=0), split)
    partner_stacked = lax.ppermute(stacked, "dc", [(c, (c + 1) % cores) for c in range(cores)])
    values = jnp.dot(stacked, weight_full, preferred_element_type=jnp.float32).astype(jnp.bfloat16)
    split_at = slot_count * seg_len
    seg_values = values[:split_at].reshape(slot_count, seg_len, kv_width)
    doc_values = values[split_at:].reshape(slot_count, mem_len, kv_width)
    doc_keys = mem_keys[0].reshape(slot_count, mem_len, kv_width)
    targets = jnp.arange(groups, dtype=jnp.int32)
    send_table = (dest_group[0][None, :] == targets[:, None]).astype(jnp.bfloat16)
    take_table = (source_group[0][:, None] == targets[None, :]).astype(jnp.bfloat16)
    out_keys = jnp.einsum(
        "hs,smc->hmc", send_table, doc_keys, preferred_element_type=jnp.float32
    ).astype(jnp.bfloat16)
    out_values = jnp.einsum(
        "hs,smc->hmc", send_table, doc_values, preferred_element_type=jnp.float32
    ).astype(jnp.bfloat16)
    in_keys, in_values = (
        lax.all_to_all(out_keys, DP_AXES, split_axis=0, concat_axis=0, tiled=True),
        lax.all_to_all(out_values, DP_AXES, split_axis=0, concat_axis=0, tiled=True),
    )
    slot_keys = jnp.einsum(
        "sh,hmc->smc", take_table, in_keys, preferred_element_type=jnp.float32
    ).astype(jnp.bfloat16)
    slot_values = jnp.einsum(
        "sh,hmc->smc", take_table, in_values, preferred_element_type=jnp.float32
    ).astype(jnp.bfloat16)
    query_slots = queries[0].reshape(slot_count, seg_len, -1)
    key_slots = keys[0].reshape(slot_count, seg_len, kv_width)
    upstream_slots = cotangent[0].reshape(slot_count, seg_len, -1)
    grad_query, slot_grad_keys, seg_grad_keys, slot_grad_values, seg_grad_values = jax.vmap(attend)(
        query_slots, key_slots, seg_values, slot_keys, slot_values, upstream_slots, lengths[0]
    )
    back_keys = jnp.einsum(
        "sh,smc->hmc",
        take_table,
        slot_grad_keys.astype(jnp.bfloat16),
        preferred_element_type=jnp.float32,
    ).astype(jnp.bfloat16)
    back_values = jnp.einsum(
        "sh,smc->hmc",
        take_table,
        slot_grad_values.astype(jnp.bfloat16),
        preferred_element_type=jnp.float32,
    ).astype(jnp.bfloat16)
    ret_keys, ret_values = (
        lax.all_to_all(back_keys, DP_AXES, split_axis=0, concat_axis=0, tiled=True),
        lax.all_to_all(back_values, DP_AXES, split_axis=0, concat_axis=0, tiled=True),
    )
    doc_grad_keys = jnp.einsum(
        "hs,hmc->smc", send_table, ret_keys, preferred_element_type=jnp.float32
    ).astype(jnp.bfloat16)
    doc_grad_values = jnp.einsum(
        "hs,hmc->smc", send_table, ret_values, preferred_element_type=jnp.float32
    ).astype(jnp.bfloat16)
    doc_grad_flat = doc_grad_values.reshape(slot_count * mem_len, kv_width)
    grad_memory = from_block_order(
        lax.dot_general(
            doc_grad_flat, weight_full, (((1,), (1,)), ((), ())), preferred_element_type=jnp.float32
        ).astype(jnp.bfloat16),
        split,
    )
    value_grads_all = jnp.concatenate(
        [seg_grad_values.astype(jnp.bfloat16).reshape(-1, kv_width), doc_grad_flat], axis=0
    )
    grads_half = lax.dynamic_slice_in_dim(value_grads_all, core * half, half, axis=1)
    swap = [(c, (c + 1) % cores) for c in range(cores)]
    partner_grads = lax.ppermute(
        lax.dynamic_slice_in_dim(value_grads_all, (1 - core) * half, half, axis=1), "dc", swap
    )
    both_rows = jnp.concatenate([stacked, partner_stacked], axis=0)
    both_grads = jnp.concatenate([grads_half, partner_grads], axis=0)
    partial = lax.dot_general(
        both_rows, both_grads, (((0,), (0,)), ((), ())), preferred_element_type=jnp.float32
    )
    shares = lax.psum_scatter(partial, "fz", scatter_dimension=0, tiled=True)
    shares = lax.psum_scatter(shares, "fy", scatter_dimension=0, tiled=True)
    shares = lax.psum_scatter(shares, "fx", scatter_dimension=0, tiled=True)
    shares = lax.psum(shares, "dx")
    grad_weight = lax.all_gather(shares, "dc", axis=1, tiled=True).astype(jnp.bfloat16)
    return (
        grad_query.reshape(1, slot_count * seg_len, -1),
        seg_grad_keys.astype(jnp.bfloat16).reshape(1, slot_count * seg_len, kv_width),
        grad_memory.reshape(1, slot_count * mem_len, model_width),
        doc_grad_keys.reshape(1, slot_count * mem_len, kv_width),
        grad_weight,
    )


def refined_mesh(mesh):
    fsdp, dp = mesh.shape["fsdp"], mesh.shape["dp"]
    devices = mesh.devices.reshape(2, fsdp // 2 // 4, 4, 2, dp // 2)
    return Mesh(devices, FSDP_AXES + DP_AXES)


def solution(mesh):
    fine = refined_mesh(mesh)
    row = P(DP_AXES, FSDP_AXES, None)
    table = P(DP_AXES, FSDP_AXES)
    in_specs = (row, row, row, row, row, row, P(FSDP_AXES, None), table, table, table)
    out_specs = (row, row, row, row, P(FSDP_AXES, None))
    return jax.shard_map(
        per_device, mesh=fine, in_specs=in_specs, out_specs=out_specs, check_vma=False
    )
```

```python
import jax
import jax.numpy as jnp
from jax import lax
from jax.sharding import Mesh, PartitionSpec as P

HEAD_DIM = 128


def attend(query_rows, seg_keys, seg_values, slot_keys, slot_values, upstream, length):
    seg_len = query_rows.shape[0]
    mem_len = slot_keys.shape[0]
    kv_width = seg_keys.shape[1]
    heads_kv = kv_width // HEAD_DIM
    group_size = query_rows.shape[1] // kv_width
    key_count = seg_len + mem_len
    all_keys = jnp.concatenate([slot_keys, seg_keys], axis=0).reshape(key_count, heads_kv, HEAD_DIM)
    all_values = jnp.concatenate([slot_values, seg_values], axis=0).reshape(
        key_count, heads_kv, HEAD_DIM
    )
    query_heads = query_rows.reshape(seg_len, heads_kv, group_size, HEAD_DIM)
    score_scale = HEAD_DIM ** (-0.5)
    scores = (
        jnp.einsum("qkgd,jkd->kgqj", query_heads, all_keys, preferred_element_type=jnp.float32)
        * score_scale
    )
    positions = jnp.arange(seg_len)[:, None]
    columns = jnp.arange(key_count)[None, :]
    visible = (columns < mem_len) | (columns - mem_len <= positions)
    scores = jnp.where(visible, scores, -1e30)
    row_max = jnp.max(scores, axis=-1, keepdims=True)
    exp_scores = jnp.exp(scores - row_max)
    weights = exp_scores / jnp.sum(exp_scores, axis=-1, keepdims=True)
    weights_low = weights.astype(jnp.bfloat16)
    output = jnp.einsum(
        "kgqj,jkd->qkgd", weights_low, all_values, preferred_element_type=jnp.float32
    ).astype(jnp.bfloat16)
    live_rows = (jnp.arange(seg_len) < length).astype(jnp.bfloat16)
    masked = (
        upstream.reshape(seg_len, heads_kv, group_size, HEAD_DIM) * live_rows[:, None, None, None]
    )
    grad_weights = jnp.einsum(
        "qkgd,jkd->kgqj", masked, all_values, preferred_element_type=jnp.float32
    )
    grad_values = jnp.einsum(
        "kgqj,qkgd->jkd", weights_low, masked, preferred_element_type=jnp.float32
    ).reshape(key_count, kv_width)
    row_delta = jnp.einsum("qkgd,qkgd->kgq", masked, output, preferred_element_type=jnp.float32)
    grad_scores = (weights * (grad_weights - row_delta[..., None]) * score_scale).astype(
        jnp.bfloat16
    )
    grad_query = (
        jnp.einsum("kgqj,jkd->qkgd", grad_scores, all_keys, preferred_element_type=jnp.float32)
        .reshape(seg_len, -1)
        .astype(jnp.bfloat16)
    )
    grad_all_keys = jnp.einsum(
        "kgqj,qkgd->jkd", grad_scores, query_heads, preferred_element_type=jnp.float32
    ).reshape(key_count, kv_width)
    return (
        grad_query,
        grad_all_keys[:mem_len],
        grad_all_keys[mem_len:],
        grad_values[:mem_len],
        grad_values[mem_len:],
    )


FSDP_AXES = ("fx", "fz", "fy")
DP_AXES = ("dx", "dc")


def to_block_order(cols, split):
    fx, fz, fy = split
    rows = cols.shape[0]
    block = cols.shape[1] // (fx * fz * fy)
    return cols.reshape(rows, fx, fz, fy, block).transpose(0, 2, 3, 1, 4).reshape(rows, -1)


def from_block_order(cols, split):
    fx, fz, fy = split
    rows = cols.shape[0]
    block = cols.shape[1] // (fx * fz * fy)
    return cols.reshape(rows, fz, fy, fx, block).transpose(0, 3, 1, 2, 4).reshape(rows, -1)


def ring_reduce_scatter(blocks, axis):
    n = blocks.shape[0]
    r = lax.axis_index(axis)
    rows = blocks.shape[1] // 2
    first, second = blocks[:, :rows], blocks[:, rows:]
    up = [(i, (i + 1) % n) for i in range(n)]
    down = [(i, (i - 1) % n) for i in range(n)]
    acc_up = first[(r - 1) % n]
    acc_down = second[(r + 1) % n]
    for step in range(n - 1):
        got_up = lax.ppermute(acc_up, axis, up)
        got_down = lax.ppermute(acc_down, axis, down)
        acc_up = got_up + first[(r - step - 2) % n]
        acc_down = got_down + second[(r + step + 2) % n]
    return jnp.concatenate([acc_up, acc_down], axis=0)


def per_device(
    tokens,
    queries,
    keys,
    memory,
    mem_keys,
    cotangent,
    value_weight,
    dest_group,
    source_group,
    lengths,
):
    split = tuple(lax.axis_size(a) for a in FSDP_AXES)
    cores = lax.axis_size("dc")
    groups = lax.axis_size("dx") * cores
    slot_count = dest_group.shape[1]
    seg_len = tokens.shape[1] // slot_count
    mem_len = memory.shape[1] // slot_count
    kv_width = value_weight.shape[1]
    model_width = tokens.shape[2]
    half = kv_width // cores
    core = lax.axis_index("dc")
    part = lax.dynamic_slice_in_dim(value_weight, core * half, half, axis=1)
    part = lax.all_gather(part, "fx", axis=0, tiled=True)
    part = lax.all_gather(part, "fy", axis=0, tiled=True)
    part = lax.all_gather(part, "fz", axis=0, tiled=True)
    other = lax.ppermute(part, "dc", [(c, (c + 1) % cores) for c in range(cores)])
    weight_full = jnp.concatenate([part, other], axis=1)

    def own_first(x):
        return jnp.where(core == 0, x, jnp.roll(x, half, axis=-1))
    stacked = to_block_order(jnp.concatenate([tokens[0], memory[0]], axis=0), split)
    partner_stacked = lax.ppermute(stacked, "dc", [(c, (c + 1) % cores) for c in range(cores)])
    values = own_first(
        jnp.dot(stacked, weight_full, preferred_element_type=jnp.float32).astype(jnp.bfloat16)
    )
    split_at = slot_count * seg_len
    seg_values = values[:split_at].reshape(slot_count, seg_len, kv_width)
    doc_values = values[split_at:].reshape(slot_count, mem_len, kv_width)
    doc_keys = mem_keys[0].reshape(slot_count, mem_len, kv_width)
    targets = jnp.arange(groups, dtype=jnp.int32)
    send_table = (dest_group[0][None, :] == targets[:, None]).astype(jnp.bfloat16)
    take_table = (source_group[0][:, None] == targets[None, :]).astype(jnp.bfloat16)
    out_keys = jnp.einsum(
        "hs,smc->hmc", send_table, doc_keys, preferred_element_type=jnp.float32
    ).astype(jnp.bfloat16)
    out_values = jnp.einsum(
        "hs,smc->hmc", send_table, doc_values, preferred_element_type=jnp.float32
    ).astype(jnp.bfloat16)
    in_keys, in_values = (
        lax.all_to_all(out_keys, DP_AXES, split_axis=0, concat_axis=0, tiled=True),
        lax.all_to_all(out_values, DP_AXES, split_axis=0, concat_axis=0, tiled=True),
    )
    slot_keys = jnp.einsum(
        "sh,hmc->smc", take_table, in_keys, preferred_element_type=jnp.float32
    ).astype(jnp.bfloat16)
    slot_values = jnp.einsum(
        "sh,hmc->smc", take_table, in_values, preferred_element_type=jnp.float32
    ).astype(jnp.bfloat16)
    query_slots = queries[0].reshape(slot_count, seg_len, -1)
    key_slots = keys[0].reshape(slot_count, seg_len, kv_width)
    upstream_slots = cotangent[0].reshape(slot_count, seg_len, -1)
    grad_query, slot_grad_keys, seg_grad_keys, slot_grad_values, seg_grad_values = jax.vmap(attend)(
        query_slots, key_slots, seg_values, slot_keys, slot_values, upstream_slots, lengths[0]
    )
    back_keys = jnp.einsum(
        "sh,smc->hmc",
        take_table,
        slot_grad_keys.astype(jnp.bfloat16),
        preferred_element_type=jnp.float32,
    ).astype(jnp.bfloat16)
    back_values = jnp.einsum(
        "sh,smc->hmc",
        take_table,
        slot_grad_values.astype(jnp.bfloat16),
        preferred_element_type=jnp.float32,
    ).astype(jnp.bfloat16)
    ret_keys, ret_values = (
        lax.all_to_all(back_keys, DP_AXES, split_axis=0, concat_axis=0, tiled=True),
        lax.all_to_all(back_values, DP_AXES, split_axis=0, concat_axis=0, tiled=True),
    )
    doc_grad_keys = jnp.einsum(
        "hs,hmc->smc", send_table, ret_keys, preferred_element_type=jnp.float32
    ).astype(jnp.bfloat16)
    doc_grad_values = jnp.einsum(
        "hs,hmc->smc", send_table, ret_values, preferred_element_type=jnp.float32
    ).astype(jnp.bfloat16)
    doc_grad_flat = doc_grad_values.reshape(slot_count * mem_len, kv_width)
    grad_memory = from_block_order(
        lax.dot_general(
            own_first(doc_grad_flat), weight_full, (((1,), (1,)), ((), ())),
            preferred_element_type=jnp.float32,
        ).astype(jnp.bfloat16),
        split,
    )
    value_grads_all = jnp.concatenate(
        [seg_grad_values.astype(jnp.bfloat16).reshape(-1, kv_width), doc_grad_flat], axis=0
    )
    grads_half = lax.dynamic_slice_in_dim(value_grads_all, core * half, half, axis=1)
    swap = [(c, (c + 1) % cores) for c in range(cores)]
    partner_grads = lax.ppermute(
        lax.dynamic_slice_in_dim(value_grads_all, (1 - core) * half, half, axis=1), "dc", swap
    )
    both_rows = jnp.concatenate([stacked, partner_stacked], axis=0)
    both_grads = jnp.concatenate([grads_half, partner_grads], axis=0)
    partial = lax.dot_general(
        both_rows, both_grads, (((0,), (0,)), ((), ())), preferred_element_type=jnp.float32
    )
    fx, fz, fy = split
    quarter = half // 2
    by_z = lax.psum_scatter(partial[:, :quarter], "fz", scatter_dimension=0, tiled=True)
    by_y = partial[:, quarter:].reshape(fz, fy, fx, -1, quarter).transpose(1, 0, 2, 3, 4)
    by_y = ring_reduce_scatter(by_y.reshape(fy, -1, quarter), "fy")
    by_z = lax.psum_scatter(by_z, "fy", scatter_dimension=0, tiled=True)
    by_y = lax.psum_scatter(by_y, "fz", scatter_dimension=0, tiled=True)
    shares = lax.psum_scatter(jnp.concatenate([by_z, by_y], axis=1), "fx", scatter_dimension=0, tiled=True)
    pairs = lax.axis_size("dx")
    shares = shares + lax.ppermute(shares, "dx", [(d, (d + 1) % pairs) for d in range(pairs)])
    shares = shares.astype(jnp.bfloat16)
    grad_weight = own_first(
        jnp.concatenate([shares, lax.ppermute(shares, "dc", swap)], axis=1)
    )
    return (
        grad_query.reshape(1, slot_count * seg_len, -1),
        seg_grad_keys.astype(jnp.bfloat16).reshape(1, slot_count * seg_len, kv_width),
        grad_memory.reshape(1, slot_count * mem_len, model_width),
        doc_grad_keys.reshape(1, slot_count * mem_len, kv_width),
        grad_weight,
    )


def refined_mesh(mesh):
    fsdp, dp = mesh.shape["fsdp"], mesh.shape["dp"]
    devices = mesh.devices.reshape(2, fsdp // 2 // 4, 4, 2, dp // 2)
    return Mesh(devices, FSDP_AXES + DP_AXES)


def solution(mesh):
    fine = refined_mesh(mesh)
    row = P(DP_AXES, FSDP_AXES, None)
    table = P(DP_AXES, FSDP_AXES)
    in_specs = (row, row, row, row, row, row, P(FSDP_AXES, None), table, table, table)
    out_specs = (row, row, row, row, P(FSDP_AXES, None))
    return jax.shard_map(
        per_device, mesh=fine, in_specs=in_specs, out_specs=out_specs, check_vma=False
    )
```

```python
import jax
import jax.numpy as jnp
from jax import lax
from jax.sharding import Mesh, PartitionSpec as P

HEAD_DIM = 128


def attend(query_rows, seg_keys, seg_values, slot_keys, slot_values, upstream, length):
    seg_len = query_rows.shape[0]
    mem_len = slot_keys.shape[0]
    kv_width = seg_keys.shape[1]
    heads_kv = kv_width // HEAD_DIM
    group_size = query_rows.shape[1] // kv_width
    key_count = seg_len + mem_len
    all_keys = jnp.concatenate([slot_keys, seg_keys], axis=0).reshape(key_count, heads_kv, HEAD_DIM)
    all_values = jnp.concatenate([slot_values, seg_values], axis=0).reshape(
        key_count, heads_kv, HEAD_DIM
    )
    query_heads = query_rows.reshape(seg_len, heads_kv, group_size, HEAD_DIM)
    score_scale = HEAD_DIM ** (-0.5)
    scores = (
        jnp.einsum("qkgd,jkd->kgqj", query_heads, all_keys, preferred_element_type=jnp.float32)
        * score_scale
    )
    positions = jnp.arange(seg_len)[:, None]
    columns = jnp.arange(key_count)[None, :]
    visible = (columns < mem_len) | (columns - mem_len <= positions)
    scores = jnp.where(visible, scores, -1e30)
    row_max = jnp.max(scores, axis=-1, keepdims=True)
    exp_scores = jnp.exp(scores - row_max)
    weights = exp_scores / jnp.sum(exp_scores, axis=-1, keepdims=True)
    weights_low = weights.astype(jnp.bfloat16)
    output = jnp.einsum(
        "kgqj,jkd->qkgd", weights_low, all_values, preferred_element_type=jnp.float32
    ).astype(jnp.bfloat16)
    live_rows = (jnp.arange(seg_len) < length).astype(jnp.bfloat16)
    masked = (
        upstream.reshape(seg_len, heads_kv, group_size, HEAD_DIM) * live_rows[:, None, None, None]
    )
    grad_weights = jnp.einsum(
        "qkgd,jkd->kgqj", masked, all_values, preferred_element_type=jnp.float32
    )
    grad_values = jnp.einsum(
        "kgqj,qkgd->jkd", weights_low, masked, preferred_element_type=jnp.float32
    ).reshape(key_count, kv_width)
    row_delta = jnp.einsum("qkgd,qkgd->kgq", masked, output, preferred_element_type=jnp.float32)
    grad_scores = (weights * (grad_weights - row_delta[..., None]) * score_scale).astype(
        jnp.bfloat16
    )
    grad_query = (
        jnp.einsum("kgqj,jkd->qkgd", grad_scores, all_keys, preferred_element_type=jnp.float32)
        .reshape(seg_len, -1)
        .astype(jnp.bfloat16)
    )
    grad_all_keys = jnp.einsum(
        "kgqj,qkgd->jkd", grad_scores, query_heads, preferred_element_type=jnp.float32
    ).reshape(key_count, kv_width)
    return (
        grad_query,
        grad_all_keys[:mem_len],
        grad_all_keys[mem_len:],
        grad_values[:mem_len],
        grad_values[mem_len:],
    )


FSDP_AXES = ("fx", "fz", "fy")
DP_AXES = ("dx", "dc")


def to_block_order(cols, split):
    fx, fz, fy = split
    rows = cols.shape[0]
    block = cols.shape[1] // (fx * fz * fy)
    return cols.reshape(rows, fx, fz, fy, block).transpose(0, 2, 3, 1, 4).reshape(rows, -1)


def from_block_order(cols, split):
    fx, fz, fy = split
    rows = cols.shape[0]
    block = cols.shape[1] // (fx * fz * fy)
    return cols.reshape(rows, fz, fy, fx, block).transpose(0, 3, 1, 2, 4).reshape(rows, -1)


def ring_all_gather(x, axis):
    n = lax.axis_size(axis)
    r = lax.axis_index(axis)
    out = lax.dynamic_update_index_in_dim(jnp.zeros((n,) + x.shape, x.dtype), x, r, 0)
    up = [(i, (i + 1) % n) for i in range(n)]
    down = [(i, (i - 1) % n) for i in range(n)]
    got = x
    for step in range(1, n // 2 + 1):
        got = lax.ppermute(got, axis, up)
        out = lax.dynamic_update_index_in_dim(out, got, (r - step) % n, 0)
    got = x
    for step in range(1, (n - 1) // 2 + 1):
        got = lax.ppermute(got, axis, down)
        out = lax.dynamic_update_index_in_dim(out, got, (r + step) % n, 0)
    return out.reshape((n * x.shape[0],) + x.shape[1:])


def per_device(
    tokens,
    queries,
    keys,
    memory,
    mem_keys,
    cotangent,
    value_weight,
    dest_group,
    source_group,
    lengths,
):
    split = tuple(lax.axis_size(a) for a in FSDP_AXES)
    cores = lax.axis_size("dc")
    groups = lax.axis_size("dx") * cores
    slot_count = dest_group.shape[1]
    seg_len = tokens.shape[1] // slot_count
    mem_len = memory.shape[1] // slot_count
    kv_width = value_weight.shape[1]
    model_width = tokens.shape[2]
    half = kv_width // cores
    core = lax.axis_index("dc")
    part = lax.dynamic_slice_in_dim(value_weight, core * half, half, axis=1)
    part = ring_all_gather(part, "fx")
    part = ring_all_gather(part, "fy")
    part = lax.all_gather(part, "fz", axis=0, tiled=True)
    other = lax.ppermute(part, "dc", [(c, (c + 1) % cores) for c in range(cores)])
    weight_full = jnp.concatenate([part, other], axis=1)

    def own_first(x):
        return jnp.where(core == 0, x, jnp.roll(x, half, axis=-1))
    stacked = to_block_order(jnp.concatenate([tokens[0], memory[0]], axis=0), split)
    partner_stacked = lax.ppermute(stacked, "dc", [(c, (c + 1) % cores) for c in range(cores)])
    values = own_first(
        jnp.dot(stacked, weight_full, preferred_element_type=jnp.float32).astype(jnp.bfloat16)
    )
    split_at = slot_count * seg_len
    seg_values = values[:split_at].reshape(slot_count, seg_len, kv_width)
    doc_values = values[split_at:].reshape(slot_count, mem_len, kv_width)
    doc_keys = mem_keys[0].reshape(slot_count, mem_len, kv_width)
    targets = jnp.arange(groups, dtype=jnp.int32)
    send_table = (dest_group[0][None, :] == targets[:, None]).astype(jnp.bfloat16)
    take_table = (source_group[0][:, None] == targets[None, :]).astype(jnp.bfloat16)
    out_keys = jnp.einsum(
        "hs,smc->hmc", send_table, doc_keys, preferred_element_type=jnp.float32
    ).astype(jnp.bfloat16)
    out_values = jnp.einsum(
        "hs,smc->hmc", send_table, doc_values, preferred_element_type=jnp.float32
    ).astype(jnp.bfloat16)
    in_keys, in_values = (
        lax.all_to_all(out_keys, DP_AXES, split_axis=0, concat_axis=0, tiled=True),
        lax.all_to_all(out_values, DP_AXES, split_axis=0, concat_axis=0, tiled=True),
    )
    slot_keys = jnp.einsum(
        "sh,hmc->smc", take_table, in_keys, preferred_element_type=jnp.float32
    ).astype(jnp.bfloat16)
    slot_values = jnp.einsum(
        "sh,hmc->smc", take_table, in_values, preferred_element_type=jnp.float32
    ).astype(jnp.bfloat16)
    query_slots = queries[0].reshape(slot_count, seg_len, -1)
    key_slots = keys[0].reshape(slot_count, seg_len, kv_width)
    upstream_slots = cotangent[0].reshape(slot_count, seg_len, -1)
    grad_query, slot_grad_keys, seg_grad_keys, slot_grad_values, seg_grad_values = jax.vmap(attend)(
        query_slots, key_slots, seg_values, slot_keys, slot_values, upstream_slots, lengths[0]
    )
    back_keys = jnp.einsum(
        "sh,smc->hmc",
        take_table,
        slot_grad_keys.astype(jnp.bfloat16),
        preferred_element_type=jnp.float32,
    ).astype(jnp.bfloat16)
    back_values = jnp.einsum(
        "sh,smc->hmc",
        take_table,
        slot_grad_values.astype(jnp.bfloat16),
        preferred_element_type=jnp.float32,
    ).astype(jnp.bfloat16)
    ret_keys, ret_values = (
        lax.all_to_all(back_keys, DP_AXES, split_axis=0, concat_axis=0, tiled=True),
        lax.all_to_all(back_values, DP_AXES, split_axis=0, concat_axis=0, tiled=True),
    )
    doc_grad_keys = jnp.einsum(
        "hs,hmc->smc", send_table, ret_keys, preferred_element_type=jnp.float32
    ).astype(jnp.bfloat16)
    doc_grad_values = jnp.einsum(
        "hs,hmc->smc", send_table, ret_values, preferred_element_type=jnp.float32
    ).astype(jnp.bfloat16)
    doc_grad_flat = doc_grad_values.reshape(slot_count * mem_len, kv_width)
    grad_memory = from_block_order(
        lax.dot_general(
            own_first(doc_grad_flat), weight_full, (((1,), (1,)), ((), ())),
            preferred_element_type=jnp.float32,
        ).astype(jnp.bfloat16),
        split,
    )
    value_grads_all = jnp.concatenate(
        [seg_grad_values.astype(jnp.bfloat16).reshape(-1, kv_width), doc_grad_flat], axis=0
    )
    grads_half = lax.dynamic_slice_in_dim(value_grads_all, core * half, half, axis=1)
    swap = [(c, (c + 1) % cores) for c in range(cores)]
    partner_grads = lax.ppermute(
        lax.dynamic_slice_in_dim(value_grads_all, (1 - core) * half, half, axis=1), "dc", swap
    )
    both_rows = jnp.concatenate([stacked, partner_stacked], axis=0)
    both_grads = jnp.concatenate([grads_half, partner_grads], axis=0)
    partial = lax.dot_general(
        both_rows, both_grads, (((0,), (0,)), ((), ())), preferred_element_type=jnp.float32
    )
    shares = lax.psum_scatter(partial, "fz", scatter_dimension=0, tiled=True)
    shares = lax.psum_scatter(shares, "fy", scatter_dimension=0, tiled=True)
    shares = lax.psum_scatter(shares, "fx", scatter_dimension=0, tiled=True)
    pairs = lax.axis_size("dx")
    shares = shares + lax.ppermute(shares, "dx", [(d, (d + 1) % pairs) for d in range(pairs)])
    shares = shares.astype(jnp.bfloat16)
    grad_weight = own_first(
        jnp.concatenate([shares, lax.ppermute(shares, "dc", swap)], axis=1)
    )
    return (
        grad_query.reshape(1, slot_count * seg_len, -1),
        seg_grad_keys.astype(jnp.bfloat16).reshape(1, slot_count * seg_len, kv_width),
        grad_memory.reshape(1, slot_count * mem_len, model_width),
        doc_grad_keys.reshape(1, slot_count * mem_len, kv_width),
        grad_weight,
    )


def refined_mesh(mesh):
    fsdp, dp = mesh.shape["fsdp"], mesh.shape["dp"]
    devices = mesh.devices.reshape(2, fsdp // 2 // 4, 4, 2, dp // 2)
    return Mesh(devices, FSDP_AXES + DP_AXES)


def solution(mesh):
    fine = refined_mesh(mesh)
    row = P(DP_AXES, FSDP_AXES, None)
    table = P(DP_AXES, FSDP_AXES)
    in_specs = (row, row, row, row, row, row, P(FSDP_AXES, None), table, table, table)
    out_specs = (row, row, row, row, P(FSDP_AXES, None))
    return jax.shard_map(
        per_device, mesh=fine, in_specs=in_specs, out_specs=out_specs, check_vma=False
    )
```

```python
import jax
import jax.numpy as jnp
from jax import lax
from jax.sharding import Mesh, PartitionSpec as P

HEAD_DIM = 128


def attend(query_rows, seg_keys, seg_values, slot_keys, slot_values, upstream, length):
    seg_len = query_rows.shape[0]
    mem_len = slot_keys.shape[0]
    kv_width = seg_keys.shape[1]
    heads_kv = kv_width // HEAD_DIM
    group_size = query_rows.shape[1] // kv_width
    key_count = seg_len + mem_len
    all_keys = jnp.concatenate([slot_keys, seg_keys], axis=0).reshape(key_count, heads_kv, HEAD_DIM)
    all_values = jnp.concatenate([slot_values, seg_values], axis=0).reshape(
        key_count, heads_kv, HEAD_DIM
    )
    query_heads = query_rows.reshape(seg_len, heads_kv, group_size, HEAD_DIM)
    score_scale = HEAD_DIM ** (-0.5)
    scores = (
        jnp.einsum("qkgd,jkd->kgqj", query_heads, all_keys, preferred_element_type=jnp.float32)
        * score_scale
    )
    positions = jnp.arange(seg_len)[:, None]
    columns = jnp.arange(key_count)[None, :]
    visible = (columns < mem_len) | (columns - mem_len <= positions)
    scores = jnp.where(visible, scores, -1e30)
    row_max = jnp.max(scores, axis=-1, keepdims=True)
    exp_scores = jnp.exp(scores - row_max)
    weights = exp_scores / jnp.sum(exp_scores, axis=-1, keepdims=True)
    weights_low = weights.astype(jnp.bfloat16)
    output = jnp.einsum(
        "kgqj,jkd->qkgd", weights_low, all_values, preferred_element_type=jnp.float32
    ).astype(jnp.bfloat16)
    live_rows = (jnp.arange(seg_len) < length).astype(jnp.bfloat16)
    masked = (
        upstream.reshape(seg_len, heads_kv, group_size, HEAD_DIM) * live_rows[:, None, None, None]
    )
    grad_weights = jnp.einsum(
        "qkgd,jkd->kgqj", masked, all_values, preferred_element_type=jnp.float32
    )
    grad_values = jnp.einsum(
        "kgqj,qkgd->jkd", weights_low, masked, preferred_element_type=jnp.float32
    ).reshape(key_count, kv_width)
    row_delta = jnp.einsum("qkgd,qkgd->kgq", masked, output, preferred_element_type=jnp.float32)
    grad_scores = (weights * (grad_weights - row_delta[..., None]) * score_scale).astype(
        jnp.bfloat16
    )
    grad_query = (
        jnp.einsum("kgqj,jkd->qkgd", grad_scores, all_keys, preferred_element_type=jnp.float32)
        .reshape(seg_len, -1)
        .astype(jnp.bfloat16)
    )
    grad_all_keys = jnp.einsum(
        "kgqj,qkgd->jkd", grad_scores, query_heads, preferred_element_type=jnp.float32
    ).reshape(key_count, kv_width)
    return (
        grad_query,
        grad_all_keys[:mem_len],
        grad_all_keys[mem_len:],
        grad_values[:mem_len],
        grad_values[mem_len:],
    )


FSDP_AXES = ("fx", "fz", "fy")
DP_AXES = ("dx", "dc")


def to_block_order(cols, split):
    fx, fz, fy = split
    rows = cols.shape[0]
    block = cols.shape[1] // (fx * fz * fy)
    return cols.reshape(rows, fx, fz, fy, block).transpose(0, 2, 3, 1, 4).reshape(rows, -1)


def from_block_order(cols, split):
    fx, fz, fy = split
    rows = cols.shape[0]
    block = cols.shape[1] // (fx * fz * fy)
    return cols.reshape(rows, fz, fy, fx, block).transpose(0, 3, 1, 2, 4).reshape(rows, -1)


def ring_all_gather(x, axis):
    n = lax.axis_size(axis)
    r = lax.axis_index(axis)
    out = lax.dynamic_update_index_in_dim(jnp.zeros((n,) + x.shape, x.dtype), x, r, 0)
    up = [(i, (i + 1) % n) for i in range(n)]
    down = [(i, (i - 1) % n) for i in range(n)]
    got = x
    for step in range(1, n // 2 + 1):
        got = lax.ppermute(got, axis, up)
        out = lax.dynamic_update_index_in_dim(out, got, (r - step) % n, 0)
    got = x
    for step in range(1, (n - 1) // 2 + 1):
        got = lax.ppermute(got, axis, down)
        out = lax.dynamic_update_index_in_dim(out, got, (r + step) % n, 0)
    return out.reshape((n * x.shape[0],) + x.shape[1:])


def per_device(
    tokens,
    queries,
    keys,
    memory,
    mem_keys,
    cotangent,
    value_weight,
    dest_group,
    source_group,
    lengths,
):
    split = tuple(lax.axis_size(a) for a in FSDP_AXES)
    cores = lax.axis_size("dc")
    groups = lax.axis_size("dx") * cores
    slot_count = dest_group.shape[1]
    seg_len = tokens.shape[1] // slot_count
    mem_len = memory.shape[1] // slot_count
    kv_width = value_weight.shape[1]
    model_width = tokens.shape[2]
    half = kv_width // cores
    core = lax.axis_index("dc")
    part = lax.dynamic_slice_in_dim(value_weight, core * half, half, axis=1)
    part = ring_all_gather(part, "fx")
    part = ring_all_gather(part, "fy")
    part = ring_all_gather(part, "fz")
    other = lax.ppermute(part, "dc", [(c, (c + 1) % cores) for c in range(cores)])
    weight_full = jnp.concatenate([part, other], axis=1)

    def own_first(x):
        return jnp.where(core == 0, x, jnp.roll(x, half, axis=-1))
    stacked = to_block_order(jnp.concatenate([tokens[0], memory[0]], axis=0), split)
    partner_stacked = lax.ppermute(stacked, "dc", [(c, (c + 1) % cores) for c in range(cores)])
    values = own_first(
        jnp.dot(stacked, weight_full, preferred_element_type=jnp.float32).astype(jnp.bfloat16)
    )
    split_at = slot_count * seg_len
    seg_values = values[:split_at].reshape(slot_count, seg_len, kv_width)
    doc_values = values[split_at:].reshape(slot_count, mem_len, kv_width)
    doc_keys = mem_keys[0].reshape(slot_count, mem_len, kv_width)
    targets = jnp.arange(groups, dtype=jnp.int32)
    send_table = (dest_group[0][None, :] == targets[:, None]).astype(jnp.bfloat16)
    take_table = (source_group[0][:, None] == targets[None, :]).astype(jnp.bfloat16)
    out_keys = jnp.einsum(
        "hs,smc->hmc", send_table, doc_keys, preferred_element_type=jnp.float32
    ).astype(jnp.bfloat16)
    out_values = jnp.einsum(
        "hs,smc->hmc", send_table, doc_values, preferred_element_type=jnp.float32
    ).astype(jnp.bfloat16)
    in_keys, in_values = (
        lax.all_to_all(out_keys, DP_AXES, split_axis=0, concat_axis=0, tiled=True),
        lax.all_to_all(out_values, DP_AXES, split_axis=0, concat_axis=0, tiled=True),
    )
    slot_keys = jnp.einsum(
        "sh,hmc->smc", take_table, in_keys, preferred_element_type=jnp.float32
    ).astype(jnp.bfloat16)
    slot_values = jnp.einsum(
        "sh,hmc->smc", take_table, in_values, preferred_element_type=jnp.float32
    ).astype(jnp.bfloat16)
    query_slots = queries[0].reshape(slot_count, seg_len, -1)
    key_slots = keys[0].reshape(slot_count, seg_len, kv_width)
    upstream_slots = cotangent[0].reshape(slot_count, seg_len, -1)
    grad_query, slot_grad_keys, seg_grad_keys, slot_grad_values, seg_grad_values = jax.vmap(attend)(
        query_slots, key_slots, seg_values, slot_keys, slot_values, upstream_slots, lengths[0]
    )
    back_keys = jnp.einsum(
        "sh,smc->hmc",
        take_table,
        slot_grad_keys.astype(jnp.bfloat16),
        preferred_element_type=jnp.float32,
    ).astype(jnp.bfloat16)
    back_values = jnp.einsum(
        "sh,smc->hmc",
        take_table,
        slot_grad_values.astype(jnp.bfloat16),
        preferred_element_type=jnp.float32,
    ).astype(jnp.bfloat16)
    ret_keys, ret_values = (
        lax.all_to_all(back_keys, DP_AXES, split_axis=0, concat_axis=0, tiled=True),
        lax.all_to_all(back_values, DP_AXES, split_axis=0, concat_axis=0, tiled=True),
    )
    doc_grad_keys = jnp.einsum(
        "hs,hmc->smc", send_table, ret_keys, preferred_element_type=jnp.float32
    ).astype(jnp.bfloat16)
    doc_grad_values = jnp.einsum(
        "hs,hmc->smc", send_table, ret_values, preferred_element_type=jnp.float32
    ).astype(jnp.bfloat16)
    doc_grad_flat = doc_grad_values.reshape(slot_count * mem_len, kv_width)
    grad_memory = from_block_order(
        lax.dot_general(
            own_first(doc_grad_flat), weight_full, (((1,), (1,)), ((), ())),
            preferred_element_type=jnp.float32,
        ).astype(jnp.bfloat16),
        split,
    )
    value_grads_all = jnp.concatenate(
        [seg_grad_values.astype(jnp.bfloat16).reshape(-1, kv_width), doc_grad_flat], axis=0
    )
    grads_half = lax.dynamic_slice_in_dim(value_grads_all, core * half, half, axis=1)
    swap = [(c, (c + 1) % cores) for c in range(cores)]
    partner_grads = lax.ppermute(
        lax.dynamic_slice_in_dim(value_grads_all, (1 - core) * half, half, axis=1), "dc", swap
    )
    both_rows = jnp.concatenate([stacked, partner_stacked], axis=0)
    both_grads = jnp.concatenate([grads_half, partner_grads], axis=0)
    partial = lax.dot_general(
        both_rows, both_grads, (((0,), (0,)), ((), ())), preferred_element_type=jnp.float32
    )
    shares = lax.psum_scatter(partial, "fz", scatter_dimension=0, tiled=True)
    shares = lax.psum_scatter(shares, "fy", scatter_dimension=0, tiled=True)
    shares = lax.psum_scatter(shares, "fx", scatter_dimension=0, tiled=True)
    pairs = lax.axis_size("dx")
    shares = shares + lax.ppermute(shares, "dx", [(d, (d + 1) % pairs) for d in range(pairs)])
    shares = shares.astype(jnp.bfloat16)
    grad_weight = own_first(
        jnp.concatenate([shares, lax.ppermute(shares, "dc", swap)], axis=1)
    )
    return (
        grad_query.reshape(1, slot_count * seg_len, -1),
        seg_grad_keys.astype(jnp.bfloat16).reshape(1, slot_count * seg_len, kv_width),
        grad_memory.reshape(1, slot_count * mem_len, model_width),
        doc_grad_keys.reshape(1, slot_count * mem_len, kv_width),
        grad_weight,
    )


def refined_mesh(mesh):
    fsdp, dp = mesh.shape["fsdp"], mesh.shape["dp"]
    devices = mesh.devices.reshape(2, fsdp // 2 // 4, 4, 2, dp // 2)
    return Mesh(devices, FSDP_AXES + DP_AXES)


def solution(mesh):
    fine = refined_mesh(mesh)
    row = P(DP_AXES, FSDP_AXES, None)
    table = P(DP_AXES, FSDP_AXES)
    in_specs = (row, row, row, row, row, row, P(FSDP_AXES, None), table, table, table)
    out_specs = (row, row, row, row, P(FSDP_AXES, None))
    return jax.shard_map(
        per_device, mesh=fine, in_specs=in_specs, out_specs=out_specs, check_vma=False
    )
```

```python
import jax
import jax.numpy as jnp
from jax import lax
from jax.sharding import Mesh, PartitionSpec as P

HEAD_DIM = 128


def attend(query_rows, seg_keys, seg_values, slot_keys, slot_values, upstream, length):
    seg_len = query_rows.shape[0]
    mem_len = slot_keys.shape[0]
    kv_width = seg_keys.shape[1]
    heads_kv = kv_width // HEAD_DIM
    group_size = query_rows.shape[1] // kv_width
    key_count = seg_len + mem_len
    all_keys = jnp.concatenate([slot_keys, seg_keys], axis=0).reshape(key_count, heads_kv, HEAD_DIM)
    all_values = jnp.concatenate([slot_values, seg_values], axis=0).reshape(
        key_count, heads_kv, HEAD_DIM
    )
    query_heads = query_rows.reshape(seg_len, heads_kv, group_size, HEAD_DIM)
    score_scale = HEAD_DIM ** (-0.5)
    scores = (
        jnp.einsum("qkgd,jkd->kgqj", query_heads, all_keys, preferred_element_type=jnp.float32)
        * score_scale
    )
    positions = jnp.arange(seg_len)[:, None]
    columns = jnp.arange(key_count)[None, :]
    visible = (columns < mem_len) | (columns - mem_len <= positions)
    scores = jnp.where(visible, scores, -1e30)
    row_max = jnp.max(scores, axis=-1, keepdims=True)
    exp_scores = jnp.exp(scores - row_max)
    weights = exp_scores / jnp.sum(exp_scores, axis=-1, keepdims=True)
    weights_low = weights.astype(jnp.bfloat16)
    output = jnp.einsum(
        "kgqj,jkd->qkgd", weights_low, all_values, preferred_element_type=jnp.float32
    ).astype(jnp.bfloat16)
    live_rows = (jnp.arange(seg_len) < length).astype(jnp.bfloat16)
    masked = (
        upstream.reshape(seg_len, heads_kv, group_size, HEAD_DIM) * live_rows[:, None, None, None]
    )
    grad_weights = jnp.einsum(
        "qkgd,jkd->kgqj", masked, all_values, preferred_element_type=jnp.float32
    )
    grad_values = jnp.einsum(
        "kgqj,qkgd->jkd", weights_low, masked, preferred_element_type=jnp.float32
    ).reshape(key_count, kv_width)
    row_delta = jnp.einsum("qkgd,qkgd->kgq", masked, output, preferred_element_type=jnp.float32)
    grad_scores = (weights * (grad_weights - row_delta[..., None]) * score_scale).astype(
        jnp.bfloat16
    )
    grad_query = (
        jnp.einsum("kgqj,jkd->qkgd", grad_scores, all_keys, preferred_element_type=jnp.float32)
        .reshape(seg_len, -1)
        .astype(jnp.bfloat16)
    )
    grad_all_keys = jnp.einsum(
        "kgqj,qkgd->jkd", grad_scores, query_heads, preferred_element_type=jnp.float32
    ).reshape(key_count, kv_width)
    return (
        grad_query,
        grad_all_keys[:mem_len],
        grad_all_keys[mem_len:],
        grad_values[:mem_len],
        grad_values[mem_len:],
    )


FSDP_AXES = ("fx", "fz", "fy")
DP_AXES = ("dx", "dc")


def to_block_order(cols, split):
    fx, fz, fy = split
    rows = cols.shape[0]
    block = cols.shape[1] // (fx * fz * fy)
    return cols.reshape(rows, fx, fz, fy, block).transpose(0, 2, 3, 1, 4).reshape(rows, -1)


def from_block_order(cols, split):
    fx, fz, fy = split
    rows = cols.shape[0]
    block = cols.shape[1] // (fx * fz * fy)
    return cols.reshape(rows, fz, fy, fx, block).transpose(0, 3, 1, 2, 4).reshape(rows, -1)


def ring_all_gather(x, axis):
    n = lax.axis_size(axis)
    r = lax.axis_index(axis)
    out = lax.dynamic_update_index_in_dim(jnp.zeros((n,) + x.shape, x.dtype), x, r, 0)
    up = [(i, (i + 1) % n) for i in range(n)]
    down = [(i, (i - 1) % n) for i in range(n)]
    got = x
    for step in range(1, n // 2 + 1):
        got = lax.ppermute(got, axis, up)
        out = lax.dynamic_update_index_in_dim(out, got, (r - step) % n, 0)
    got = x
    for step in range(1, (n - 1) // 2 + 1):
        got = lax.ppermute(got, axis, down)
        out = lax.dynamic_update_index_in_dim(out, got, (r + step) % n, 0)
    return out.reshape((n * x.shape[0],) + x.shape[1:])


def per_device(
    tokens,
    queries,
    keys,
    memory,
    mem_keys,
    cotangent,
    value_weight,
    dest_group,
    source_group,
    lengths,
):
    split = tuple(lax.axis_size(a) for a in FSDP_AXES)
    cores = lax.axis_size("dc")
    groups = lax.axis_size("dx") * cores
    slot_count = dest_group.shape[1]
    seg_len = tokens.shape[1] // slot_count
    mem_len = memory.shape[1] // slot_count
    kv_width = value_weight.shape[1]
    model_width = tokens.shape[2]
    half = kv_width // cores
    core = lax.axis_index("dc")
    part = lax.dynamic_slice_in_dim(value_weight, core * half, half, axis=1)
    part = ring_all_gather(part, "fx")
    part = ring_all_gather(part, "fy")
    part = lax.all_gather(part, "fz", axis=0, tiled=True)
    other = lax.ppermute(part, "dc", [(c, (c + 1) % cores) for c in range(cores)])
    weight_full = jnp.concatenate([part, other], axis=1)

    def own_first(x):
        return jnp.where(core == 0, x, jnp.roll(x, half, axis=-1))
    stacked = to_block_order(jnp.concatenate([tokens[0], memory[0]], axis=0), split)
    partner_stacked = lax.ppermute(stacked, "dc", [(c, (c + 1) % cores) for c in range(cores)])
    values = own_first(
        jnp.dot(stacked, weight_full, preferred_element_type=jnp.float32).astype(jnp.bfloat16)
    )
    split_at = slot_count * seg_len
    seg_values = values[:split_at].reshape(slot_count, seg_len, kv_width)
    doc_values = values[split_at:].reshape(slot_count, mem_len, kv_width)
    doc_keys = mem_keys[0].reshape(slot_count, mem_len, kv_width)
    targets = jnp.arange(groups, dtype=jnp.int32)
    send_table = (dest_group[0][None, :] == targets[:, None]).astype(jnp.bfloat16)
    take_table = (source_group[0][:, None] == targets[None, :]).astype(jnp.bfloat16)
    out_keys = jnp.einsum(
        "hs,smc->hmc", send_table, doc_keys, preferred_element_type=jnp.float32
    ).astype(jnp.bfloat16)
    out_values = jnp.einsum(
        "hs,smc->hmc", send_table, doc_values, preferred_element_type=jnp.float32
    ).astype(jnp.bfloat16)
    in_keys, in_values = (
        lax.all_to_all(out_keys, DP_AXES, split_axis=0, concat_axis=0, tiled=True),
        lax.all_to_all(out_values, DP_AXES, split_axis=0, concat_axis=0, tiled=True),
    )
    slot_keys = jnp.einsum(
        "sh,hmc->smc", take_table, in_keys, preferred_element_type=jnp.float32
    ).astype(jnp.bfloat16)
    slot_values = jnp.einsum(
        "sh,hmc->smc", take_table, in_values, preferred_element_type=jnp.float32
    ).astype(jnp.bfloat16)
    query_slots = queries[0].reshape(slot_count, seg_len, -1)
    key_slots = keys[0].reshape(slot_count, seg_len, kv_width)
    upstream_slots = cotangent[0].reshape(slot_count, seg_len, -1)
    grad_query, slot_grad_keys, seg_grad_keys, slot_grad_values, seg_grad_values = jax.vmap(attend)(
        query_slots, key_slots, seg_values, slot_keys, slot_values, upstream_slots, lengths[0]
    )
    back_keys = jnp.einsum(
        "sh,smc->hmc",
        take_table,
        slot_grad_keys.astype(jnp.bfloat16),
        preferred_element_type=jnp.float32,
    ).astype(jnp.bfloat16)
    back_values = jnp.einsum(
        "sh,smc->hmc",
        take_table,
        slot_grad_values.astype(jnp.bfloat16),
        preferred_element_type=jnp.float32,
    ).astype(jnp.bfloat16)
    ret_keys, ret_values = (
        lax.all_to_all(back_keys, DP_AXES, split_axis=0, concat_axis=0, tiled=True),
        lax.all_to_all(back_values, DP_AXES, split_axis=0, concat_axis=0, tiled=True),
    )
    doc_grad_keys = jnp.einsum(
        "hs,hmc->smc", send_table, ret_keys, preferred_element_type=jnp.float32
    ).astype(jnp.bfloat16)
    doc_grad_values = jnp.einsum(
        "hs,hmc->smc", send_table, ret_values, preferred_element_type=jnp.float32
    ).astype(jnp.bfloat16)
    doc_grad_flat = doc_grad_values.reshape(slot_count * mem_len, kv_width)
    grad_memory = from_block_order(
        lax.dot_general(
            own_first(doc_grad_flat), weight_full, (((1,), (1,)), ((), ())),
            preferred_element_type=jnp.float32,
        ).astype(jnp.bfloat16),
        split,
    )
    value_grads_all = jnp.concatenate(
        [seg_grad_values.astype(jnp.bfloat16).reshape(-1, kv_width), doc_grad_flat], axis=0
    )
    grads_half = lax.dynamic_slice_in_dim(value_grads_all, core * half, half, axis=1)
    swap = [(c, (c + 1) % cores) for c in range(cores)]
    partner_grads = lax.ppermute(
        lax.dynamic_slice_in_dim(value_grads_all, (1 - core) * half, half, axis=1), "dc", swap
    )
    both_rows = jnp.concatenate([stacked, partner_stacked], axis=0)
    both_grads = jnp.concatenate([grads_half, partner_grads], axis=0)
    partial = lax.dot_general(
        both_rows, both_grads, (((0,), (0,)), ((), ())), preferred_element_type=jnp.float32
    )
    shares = lax.psum_scatter(partial, "fz", scatter_dimension=0, tiled=True)
    shares = lax.psum_scatter(shares, "fy", scatter_dimension=0, tiled=True)
    links = lax.axis_size("fx")
    at = lax.axis_index("fx")
    blocks = shares.reshape(links, -1, shares.shape[1])
    shares = blocks[at] + lax.ppermute(
        blocks[(at + 1) % links], "fx", [(d, (d + 1) % links) for d in range(links)]
    )
    pairs = lax.axis_size("dx")
    shares = shares + lax.ppermute(shares, "dx", [(d, (d + 1) % pairs) for d in range(pairs)])
    shares = shares.astype(jnp.bfloat16)
    grad_weight = own_first(
        jnp.concatenate([shares, lax.ppermute(shares, "dc", swap)], axis=1)
    )
    return (
        grad_query.reshape(1, slot_count * seg_len, -1),
        seg_grad_keys.astype(jnp.bfloat16).reshape(1, slot_count * seg_len, kv_width),
        grad_memory.reshape(1, slot_count * mem_len, model_width),
        doc_grad_keys.reshape(1, slot_count * mem_len, kv_width),
        grad_weight,
    )


def refined_mesh(mesh):
    fsdp, dp = mesh.shape["fsdp"], mesh.shape["dp"]
    devices = mesh.devices.reshape(2, fsdp // 2 // 4, 4, 2, dp // 2)
    return Mesh(devices, FSDP_AXES + DP_AXES)


def solution(mesh):
    fine = refined_mesh(mesh)
    row = P(DP_AXES, FSDP_AXES, None)
    table = P(DP_AXES, FSDP_AXES)
    in_specs = (row, row, row, row, row, row, P(FSDP_AXES, None), table, table, table)
    out_specs = (row, row, row, row, P(FSDP_AXES, None))
    return jax.shard_map(
        per_device, mesh=fine, in_specs=in_specs, out_specs=out_specs, check_vma=False
    )
```

```python
import jax
import jax.numpy as jnp
from jax import lax
from jax.sharding import Mesh, PartitionSpec as P

HEAD_DIM = 128


def attend(query_rows, seg_keys, seg_values, slot_keys, slot_values, upstream, length):
    seg_len = query_rows.shape[0]
    mem_len = slot_keys.shape[0]
    kv_width = seg_keys.shape[1]
    heads_kv = kv_width // HEAD_DIM
    group_size = query_rows.shape[1] // kv_width
    key_count = seg_len + mem_len
    all_keys = jnp.concatenate([slot_keys, seg_keys], axis=0).reshape(key_count, heads_kv, HEAD_DIM)
    all_values = jnp.concatenate([slot_values, seg_values], axis=0).reshape(
        key_count, heads_kv, HEAD_DIM
    )
    query_heads = query_rows.reshape(seg_len, heads_kv, group_size, HEAD_DIM)
    score_scale = HEAD_DIM ** (-0.5)
    scores = (
        jnp.einsum("qkgd,jkd->kgqj", query_heads, all_keys, preferred_element_type=jnp.float32)
        * score_scale
    )
    positions = jnp.arange(seg_len)[:, None]
    columns = jnp.arange(key_count)[None, :]
    visible = (columns < mem_len) | (columns - mem_len <= positions)
    scores = jnp.where(visible, scores, -1e30)
    row_max = jnp.max(scores, axis=-1, keepdims=True)
    exp_scores = jnp.exp(scores - row_max)
    weights = exp_scores / jnp.sum(exp_scores, axis=-1, keepdims=True)
    weights_low = weights.astype(jnp.bfloat16)
    output = jnp.einsum(
        "kgqj,jkd->qkgd", weights_low, all_values, preferred_element_type=jnp.float32
    ).astype(jnp.bfloat16)
    live_rows = (jnp.arange(seg_len) < length).astype(jnp.bfloat16)
    masked = (
        upstream.reshape(seg_len, heads_kv, group_size, HEAD_DIM) * live_rows[:, None, None, None]
    )
    grad_weights = jnp.einsum(
        "qkgd,jkd->kgqj", masked, all_values, preferred_element_type=jnp.float32
    )
    grad_values = jnp.einsum(
        "kgqj,qkgd->jkd", weights_low, masked, preferred_element_type=jnp.float32
    ).reshape(key_count, kv_width)
    row_delta = jnp.einsum("qkgd,qkgd->kgq", masked, output, preferred_element_type=jnp.float32)
    grad_scores = (weights * (grad_weights - row_delta[..., None]) * score_scale).astype(
        jnp.bfloat16
    )
    grad_query = (
        jnp.einsum("kgqj,jkd->qkgd", grad_scores, all_keys, preferred_element_type=jnp.float32)
        .reshape(seg_len, -1)
        .astype(jnp.bfloat16)
    )
    grad_all_keys = jnp.einsum(
        "kgqj,qkgd->jkd", grad_scores, query_heads, preferred_element_type=jnp.float32
    ).reshape(key_count, kv_width)
    return (
        grad_query,
        grad_all_keys[:mem_len],
        grad_all_keys[mem_len:],
        grad_values[:mem_len],
        grad_values[mem_len:],
    )


FSDP_AXES = ("fx", "fz", "fy")
DP_AXES = ("dx", "dc")


def to_block_order(cols, split):
    fx, fz, fy = split
    rows = cols.shape[0]
    block = cols.shape[1] // (fx * fz * fy)
    return cols.reshape(rows, fx, fz, fy, block).transpose(0, 2, 3, 1, 4).reshape(rows, -1)


def from_block_order(cols, split):
    fx, fz, fy = split
    rows = cols.shape[0]
    block = cols.shape[1] // (fx * fz * fy)
    return cols.reshape(rows, fz, fy, fx, block).transpose(0, 3, 1, 2, 4).reshape(rows, -1)


def ring_all_gather(x, axis):
    n = lax.axis_size(axis)
    r = lax.axis_index(axis)
    out = lax.dynamic_update_index_in_dim(jnp.zeros((n,) + x.shape, x.dtype), x, r, 0)
    up = [(i, (i + 1) % n) for i in range(n)]
    down = [(i, (i - 1) % n) for i in range(n)]
    got = x
    for step in range(1, n // 2 + 1):
        got = lax.ppermute(got, axis, up)
        out = lax.dynamic_update_index_in_dim(out, got, (r - step) % n, 0)
    got = x
    for step in range(1, (n - 1) // 2 + 1):
        got = lax.ppermute(got, axis, down)
        out = lax.dynamic_update_index_in_dim(out, got, (r + step) % n, 0)
    return out.reshape((n * x.shape[0],) + x.shape[1:])


def ring_reduce_scatter(blocks, axis):
    n = blocks.shape[0]
    r = lax.axis_index(axis)
    rows = blocks.shape[1] // 2
    first, second = blocks[:, :rows], blocks[:, rows:]
    up = [(i, (i + 1) % n) for i in range(n)]
    down = [(i, (i - 1) % n) for i in range(n)]
    acc_up = first[(r - 1) % n]
    acc_down = second[(r + 1) % n]
    for step in range(n - 1):
        got_up = lax.ppermute(acc_up, axis, up)
        got_down = lax.ppermute(acc_down, axis, down)
        acc_up = got_up + first[(r - step - 2) % n]
        acc_down = got_down + second[(r + step + 2) % n]
    return jnp.concatenate([acc_up, acc_down], axis=0)


def per_device(
    tokens,
    queries,
    keys,
    memory,
    mem_keys,
    cotangent,
    value_weight,
    dest_group,
    source_group,
    lengths,
):
    split = tuple(lax.axis_size(a) for a in FSDP_AXES)
    cores = lax.axis_size("dc")
    groups = lax.axis_size("dx") * cores
    slot_count = dest_group.shape[1]
    seg_len = tokens.shape[1] // slot_count
    mem_len = memory.shape[1] // slot_count
    kv_width = value_weight.shape[1]
    model_width = tokens.shape[2]
    half = kv_width // cores
    core = lax.axis_index("dc")
    part = lax.dynamic_slice_in_dim(value_weight, core * half, half, axis=1)
    part = ring_all_gather(part, "fx")
    part = ring_all_gather(part, "fy")
    part = lax.all_gather(part, "fz", axis=0, tiled=True)
    other = lax.ppermute(part, "dc", [(c, (c + 1) % cores) for c in range(cores)])
    weight_full = jnp.concatenate([part, other], axis=1)

    def own_first(x):
        return jnp.where(core == 0, x, jnp.roll(x, half, axis=-1))
    stacked = to_block_order(jnp.concatenate([tokens[0], memory[0]], axis=0), split)
    partner_stacked = lax.ppermute(stacked, "dc", [(c, (c + 1) % cores) for c in range(cores)])
    values = own_first(
        jnp.dot(stacked, weight_full, preferred_element_type=jnp.float32).astype(jnp.bfloat16)
    )
    split_at = slot_count * seg_len
    seg_values = values[:split_at].reshape(slot_count, seg_len, kv_width)
    doc_values = values[split_at:].reshape(slot_count, mem_len, kv_width)
    doc_keys = mem_keys[0].reshape(slot_count, mem_len, kv_width)
    targets = jnp.arange(groups, dtype=jnp.int32)
    send_table = (dest_group[0][None, :] == targets[:, None]).astype(jnp.bfloat16)
    take_table = (source_group[0][:, None] == targets[None, :]).astype(jnp.bfloat16)
    out_keys = jnp.einsum(
        "hs,smc->hmc", send_table, doc_keys, preferred_element_type=jnp.float32
    ).astype(jnp.bfloat16)
    out_values = jnp.einsum(
        "hs,smc->hmc", send_table, doc_values, preferred_element_type=jnp.float32
    ).astype(jnp.bfloat16)
    in_keys, in_values = (
        lax.all_to_all(out_keys, DP_AXES, split_axis=0, concat_axis=0, tiled=True),
        lax.all_to_all(out_values, DP_AXES, split_axis=0, concat_axis=0, tiled=True),
    )
    slot_keys = jnp.einsum(
        "sh,hmc->smc", take_table, in_keys, preferred_element_type=jnp.float32
    ).astype(jnp.bfloat16)
    slot_values = jnp.einsum(
        "sh,hmc->smc", take_table, in_values, preferred_element_type=jnp.float32
    ).astype(jnp.bfloat16)
    query_slots = queries[0].reshape(slot_count, seg_len, -1)
    key_slots = keys[0].reshape(slot_count, seg_len, kv_width)
    upstream_slots = cotangent[0].reshape(slot_count, seg_len, -1)
    grad_query, slot_grad_keys, seg_grad_keys, slot_grad_values, seg_grad_values = jax.vmap(attend)(
        query_slots, key_slots, seg_values, slot_keys, slot_values, upstream_slots, lengths[0]
    )
    back_keys = jnp.einsum(
        "sh,smc->hmc",
        take_table,
        slot_grad_keys.astype(jnp.bfloat16),
        preferred_element_type=jnp.float32,
    ).astype(jnp.bfloat16)
    back_values = jnp.einsum(
        "sh,smc->hmc",
        take_table,
        slot_grad_values.astype(jnp.bfloat16),
        preferred_element_type=jnp.float32,
    ).astype(jnp.bfloat16)
    ret_keys, ret_values = (
        lax.all_to_all(back_keys, DP_AXES, split_axis=0, concat_axis=0, tiled=True),
        lax.all_to_all(back_values, DP_AXES, split_axis=0, concat_axis=0, tiled=True),
    )
    doc_grad_keys = jnp.einsum(
        "hs,hmc->smc", send_table, ret_keys, preferred_element_type=jnp.float32
    ).astype(jnp.bfloat16)
    doc_grad_values = jnp.einsum(
        "hs,hmc->smc", send_table, ret_values, preferred_element_type=jnp.float32
    ).astype(jnp.bfloat16)
    doc_grad_flat = doc_grad_values.reshape(slot_count * mem_len, kv_width)
    grad_memory = from_block_order(
        lax.dot_general(
            own_first(doc_grad_flat), weight_full, (((1,), (1,)), ((), ())),
            preferred_element_type=jnp.float32,
        ).astype(jnp.bfloat16),
        split,
    )
    value_grads_all = jnp.concatenate(
        [seg_grad_values.astype(jnp.bfloat16).reshape(-1, kv_width), doc_grad_flat], axis=0
    )
    grads_half = lax.dynamic_slice_in_dim(value_grads_all, core * half, half, axis=1)
    swap = [(c, (c + 1) % cores) for c in range(cores)]
    partner_grads = lax.ppermute(
        lax.dynamic_slice_in_dim(value_grads_all, (1 - core) * half, half, axis=1), "dc", swap
    )
    both_rows = jnp.concatenate([stacked, partner_stacked], axis=0)
    both_grads = jnp.concatenate([grads_half, partner_grads], axis=0)
    partial = lax.dot_general(
        both_rows, both_grads, (((0,), (0,)), ((), ())), preferred_element_type=jnp.float32
    )
    shares = lax.psum_scatter(partial, "fz", scatter_dimension=0, tiled=True)
    shares = ring_reduce_scatter(shares.reshape(lax.axis_size("fy"), -1, shares.shape[1]), "fy")
    links = lax.axis_size("fx")
    at = lax.axis_index("fx")
    blocks = shares.reshape(links, -1, shares.shape[1])
    shares = blocks[at] + lax.ppermute(
        blocks[(at + 1) % links], "fx", [(d, (d + 1) % links) for d in range(links)]
    )
    pairs = lax.axis_size("dx")
    shares = shares + lax.ppermute(shares, "dx", [(d, (d + 1) % pairs) for d in range(pairs)])
    shares = shares.astype(jnp.bfloat16)
    grad_weight = own_first(
        jnp.concatenate([shares, lax.ppermute(shares, "dc", swap)], axis=1)
    )
    return (
        grad_query.reshape(1, slot_count * seg_len, -1),
        seg_grad_keys.astype(jnp.bfloat16).reshape(1, slot_count * seg_len, kv_width),
        grad_memory.reshape(1, slot_count * mem_len, model_width),
        doc_grad_keys.reshape(1, slot_count * mem_len, kv_width),
        grad_weight,
    )


def refined_mesh(mesh):
    fsdp, dp = mesh.shape["fsdp"], mesh.shape["dp"]
    devices = mesh.devices.reshape(2, fsdp // 2 // 4, 4, 2, dp // 2)
    return Mesh(devices, FSDP_AXES + DP_AXES)


def solution(mesh):
    fine = refined_mesh(mesh)
    row = P(DP_AXES, FSDP_AXES, None)
    table = P(DP_AXES, FSDP_AXES)
    in_specs = (row, row, row, row, row, row, P(FSDP_AXES, None), table, table, table)
    out_specs = (row, row, row, row, P(FSDP_AXES, None))
    return jax.shard_map(
        per_device, mesh=fine, in_specs=in_specs, out_specs=out_specs, check_vma=False
    )
```
